128 devices in a mesh: row: 4 (over y), vocab: 32 (over z, x, core).
Axes of the slice: x: 4, y: 4, z: 4, core: 2. Of those that a mesh axis runs over, the one named last changes fastest.
Arguments:
- tokens: bfloat16 [1280, 7168], P(('row', 'vocab')), may hold values from -60 to 60
- norm_gain: float32 [7168], replicated, may hold values from 0.5 to 1.5
- router: bfloat16 [7168, 32], replicated, may hold values from -0.0625 to 0.0625
- routes: int32 [1280, 8], P(('row', 'vocab')), may hold values from 0 to 31, all different within a row; in each aligned block of 10 rows (0 to 9, 10 to 19, ...) at most 3 rows name the same one
- w_gate: bfloat16 [32, 7168, 1024], P('vocab', None, 'row'), may hold values from -0.0625 to 0.0625
- w_up: bfloat16 [32, 7168, 1024], P('vocab', None, 'row'), may hold values from -0.0625 to 0.0625
- w_down: bfloat16 [32, 1024, 7168], P('vocab', 'row'), may hold values from -0.1875 to 0.1875
- head_gain: float32 [7168], replicated, may hold values from 0.5 to 1.5
- head: bfloat16 [65536, 7168], P(('row', 'vocab')), may hold values from -0.18 to 0.18
- draft_logits: bfloat16 [256, 4, 65536], P(None, None, ('row', 'vocab')), may hold values from -18 to 235
- draft_tokens: int32 [256, 4], replicated, may hold values from 0 to 65535
- reject_pos: int32 [256], replicated, may hold values from 0 to 4
Outputs:
- residual: float32 [256, 65536], P(None, ('row', 'vocab'))
- accept: float32 [256, 4], replicated
The draws below stay inside these ranges and needn't reach their ends.
Inputs may be any that keep to these rules, and one draw needn't show every extreme that they name: `routes`: each row names 8 different experts. Among the rows of one device no expert is named more than 3 times, and some device's rows name some expert exactly 3 times.
All inputs are finite; a program needn't handle non-finite values.
Results may differ from the reference program's by a relative error of at most 0.012.
Values may be sent and summed in bfloat16 or wider, within the bound.
No kernel may reach another device: no remote copies, remote signals or barrier semaphores. Data moves between devices by JAX's collectives and lax.ppermute only.
A program may use at most 256 MiB of HBM per device.

```python
import math
import jax
import jax.numpy as jnp
import numpy as np
from jax import lax

D = 7168
FF = 1024
V = 65536
TOP = 8
DRAFTS = 4
SLOTS = 5
ROWS_DEV = 10
REQ = 256
ROWS = 1280
EXPERTS = 32
CAP = 3
N_ROW = 4
N_VOCAB = 32


def reject_helper(key):
    return jax.random.randint(jax.random.fold_in(key, 31), (REQ,), 0, DRAFTS + 1)


def draw_reject_pos(key, part):
    return reject_helper(key).astype(jnp.int32)


def draw_tokens(key, part):
    base_vals = jax.random.normal(jax.random.fold_in(key, 1), (ROWS, D))
    row_scale = jnp.exp(jax.random.uniform(jax.random.fold_in(key, 2), (ROWS, 1), minval=math.log(0.5), maxval=math.log(5.0)))
    col_scale = jnp.exp(jax.random.uniform(jax.random.fold_in(key, 3), (1, D), minval=math.log(0.4), maxval=math.log(2.5)))
    values = jnp.clip(base_vals * row_scale * col_scale, -60.0, 60.0)
    return values.astype(jnp.bfloat16)


def draw_head(key, part):
    spread = 3.0 / math.sqrt(D)
    base_vals = jax.random.normal(jax.random.fold_in(key, 11), (V, D)) * spread
    return jnp.clip(base_vals, -0.18, 0.18).astype(jnp.bfloat16)


def draw_draft_logits(key, part):
    base_vals = jnp.clip(3.0 * jax.random.normal(jax.random.fold_in(key, 21), (REQ, DRAFTS, V)), -18.0, 18.0)
    return base_vals.astype(jnp.bfloat16)


def plant(result, own_key, smallest, high):
    shape = result.shape
    place = [jax.random.randint(jax.random.fold_in(own_key, axis), (), 0, shape[axis]) for axis in range(len(shape))]
    result = result.at[tuple(place)].set(smallest)
    longest = shape.index(max(shape))
    place[longest] = (place[longest] + 1) % shape[longest]
    return result.at[tuple(place)].set(high)


def levels(own_key, shape, cuts, least, top_value):
    level = 1.0
    for dim, shards_of in cuts:
        draws = jax.random.uniform(jax.random.fold_in(jax.random.fold_in(own_key, 6), dim), (shards_of,), jnp.float32, least / len(cuts), top_value / len(cuts))
        level = level * jnp.repeat(jnp.exp(draws), shape[dim] // shards_of).reshape((-1,) + (1,) * (len(shape) - 1 - dim))
    return level


def shared_out(stream_key, own, number, rows, number_of, top, most, slope):
    order = jax.random.permutation(stream_key, number_of)
    heavy_load, usual = load_shares(number_of, rows * top, most, slope, True), load_shares(number_of, rows * top, most, slope, False)
    places = jnp.arange(number_of)

    def named(tallies, offset_by):
        used = int((tallies > 0).sum())
        fixed = max(1, used // 4)
        shifted = fixed + (places - fixed + offset_by * (used - fixed)) % max(1, number_of - fixed)
        return jnp.zeros((number_of,), jnp.int32).at[order[jnp.where(places < fixed, places, shifted)]].set(jnp.asarray(tallies, jnp.int32))

    tallies = jnp.where(number % 4 == 0, named(heavy_load, number // 4), named(usual, number - number // 4 - 1))
    mixed = jax.random.permutation(jax.random.fold_in(own, 3), number_of)
    donor, sink = mixed[0:number_of // 2 * 2:2], mixed[1:number_of // 2 * 2:2]
    slack = jnp.minimum(tallies[donor] - 1, most - tallies[sink]) // 2
    slack = jnp.where((donor == order[0]) | (sink == order[0]) | (tallies[sink] == 0), 0, jnp.maximum(slack, 0))
    shifted = jax.random.randint(jax.random.fold_in(own, 4), (number_of // 2,), 0, 1 << 20) % (slack + 1)
    tallies = tallies.at[donor].add(-shifted).at[sink].add(shifted)
    members = jnp.searchsorted(jnp.cumsum(tallies), jnp.arange(rows * top), side="right").astype(jnp.int32)
    table = members.reshape(top, rows).T
    table = table[jax.random.permutation(jax.random.fold_in(own, 1), rows)]
    offset_by = jax.random.randint(jax.random.fold_in(own, 2), (rows, 1), 0, top)
    return jnp.take_along_axis(table, (jnp.arange(top)[None, :] + offset_by) % top, axis=1)


def load_shares(amount, total, most, slope, full):
    portions = [(1 << 20) // math.isqrt(grade ** slope) + 1 for grade in range(1, amount + 1)]
    largest = most if full else min(most, max(-(-total // amount), total * portions[0] // sum(portions)))
    least = 1 if total - largest >= amount - 1 else 0
    given, spare = [largest] + [least] * (amount - 1), total - largest - least * (amount - 1)
    while spare > 0:
        candidates = [i for i in range(1, amount) if given[i] < largest] or [i for i in range(1, amount) if given[i] < most]
        pool, budget = sum([portions[i] for i in candidates]), spare
        for i in candidates:
            more = min(most - given[i], max(1, budget * portions[i] // pool), spare)
            given[i] = given[i] + more
            spare = spare - more
    return np.array(given)


def centred(key, shape, deviation, most, split=(), kind=jnp.bfloat16):
    level = levels(key, shape, split, -0.22, 0.18) if split else 1.0
    drawn = jax.random.normal(key, shape, jnp.float32) * deviation * level
    return jnp.minimum(jnp.maximum(drawn, -most), most).astype(kind)


def setup_inputs(seed: int = 0) -> dict:
    splits = jax.random.split(jax.random.key(seed), 13)
    tokens = draw_tokens(jax.random.fold_in(splits[12], 71), 0)
    norm_gain = jnp.clip(1.0 + 0.1 * jax.random.normal(splits[1], (D,), jnp.float32), 0.5, 1.5)
    router = centred(splits[2], (D, EXPERTS), D ** -0.5, 0.0625)
    routes_keys = jax.random.split(jax.random.fold_in(splits[3], 1), ROWS // ROWS_DEV)
    routes_turns = jax.random.permutation(jax.random.fold_in(splits[3], 3), ROWS // ROWS_DEV)
    routes = jax.vmap(lambda own, number: shared_out(jax.random.fold_in(splits[3], 2), own, number, ROWS_DEV, EXPERTS, TOP, CAP, 1))(routes_keys, routes_turns).reshape((ROWS, TOP))
    w_gate = centred(splits[4], (EXPERTS, D, FF), D ** -0.5, 0.0625, ((0, 32), (2, 4)))
    w_up = centred(splits[5], (EXPERTS, D, FF), D ** -0.5, 0.0625, ((0, 32), (2, 4)))
    w_down = centred(splits[6], (EXPERTS, FF, D), FF ** -0.5, 0.1875, ((0, 32), (1, 4)))
    head_gain = jnp.clip(1.0 + 0.1 * jax.random.normal(splits[7], (D,), jnp.float32), 0.5, 1.5)
    head = draw_head(jax.random.fold_in(splits[12], 71), 0)
    draft_logits = draw_draft_logits(jax.random.fold_in(splits[12], 71), 0)
    draft_tokens = plant(jax.random.randint(splits[10], (REQ, DRAFTS), 0, V), jax.random.fold_in(splits[10], 1), 0, V - 1).astype(jnp.int32)
    reject_pos = draw_reject_pos(jax.random.fold_in(splits[12], 71), 0)
    return dict(tokens=tokens, norm_gain=norm_gain, router=router, routes=routes, w_gate=w_gate, w_up=w_up, w_down=w_down, head_gain=head_gain, head=head, draft_logits=draft_logits, draft_tokens=draft_tokens, reject_pos=reject_pos)


def rms_norm(values, gain):
    return values * lax.rsqrt(lax.optimization_barrier(jnp.mean(values * values, axis=-1, keepdims=True)) + 1e-06) * gain

def reference(tokens, norm_gain, router, routes, w_gate, w_up, w_down, head_gain, head, draft_logits, draft_tokens, reject_pos):
    resid_in = tokens.astype(jnp.float32)
    normed = rms_norm(resid_in, norm_gain).astype(jnp.bfloat16)
    scores = jax.nn.sigmoid(jnp.dot(normed, router, preferred_element_type=jnp.float32))
    picked = jnp.take_along_axis(scores, routes, axis=1)
    weights = 2.5 * picked / lax.optimization_barrier(jnp.sum(picked, axis=1, keepdims=True))
    ff_part = FF // N_ROW
    most_rows = min(ROWS, CAP * N_ROW * N_VOCAB)

    def one_expert(moe_sum, expert):
        hit_mask = routes == expert
        named_rows = jnp.any(hit_mask, axis=1)
        row_idx = jnp.nonzero(named_rows, size=most_rows, fill_value=0)[0].astype(jnp.int32)
        valid_rows = (jnp.arange(most_rows) < jnp.sum(named_rows.astype(jnp.int32))).astype(jnp.float32)
        chosen = normed[row_idx]
        gate_out = jnp.dot(chosen, w_gate[expert], preferred_element_type=jnp.float32)
        up_out = jnp.dot(chosen, w_up[expert], preferred_element_type=jnp.float32)
        hidden = (jax.nn.silu(gate_out) * up_out).astype(jnp.bfloat16)
        down_all = w_down[expert]
        part_sum = jnp.zeros((most_rows, D), jnp.float32)
        for block in range(N_ROW):
            part_term = jnp.dot(hidden[:, block * ff_part:(block + 1) * ff_part], down_all[block * ff_part:(block + 1) * ff_part], preferred_element_type=jnp.float32).astype(jnp.bfloat16)
            part_term = lax.optimization_barrier(part_term)
            part_sum = part_sum + part_term.astype(jnp.float32)
        expert_out = lax.optimization_barrier(part_sum.astype(jnp.bfloat16)).astype(jnp.float32)
        row_weight = lax.optimization_barrier(jnp.sum(jnp.where(hit_mask, weights, 0.0), axis=1))[row_idx] * valid_rows
        return (moe_sum.at[row_idx].add(row_weight[:, None] * expert_out), None)
    moe_sum, _ = lax.scan(one_expert, jnp.zeros((ROWS, D), jnp.float32), jnp.arange(EXPERTS, dtype=jnp.int32))
    mixed_rows = resid_in + moe_sum
    final_normed = rms_norm(mixed_rows, head_gain).astype(jnp.bfloat16)
    logits = lax.dot_general(final_normed, head, (((1,), (1,)), ((), ())), preferred_element_type=jnp.float32)
    logits = logits.reshape(REQ, SLOTS, V)
    top_target = lax.optimization_barrier(jnp.max(logits, axis=-1, keepdims=True))
    sum_target = lax.optimization_barrier(jnp.sum(jnp.exp(logits - top_target), axis=-1, keepdims=True))
    target = jnp.exp(logits - top_target) / sum_target
    draft_vals = draft_logits.astype(jnp.float32)
    top_draft = lax.optimization_barrier(jnp.max(draft_vals, axis=-1, keepdims=True))
    sum_draft = lax.optimization_barrier(jnp.sum(jnp.exp(draft_vals - top_draft), axis=-1, keepdims=True))
    draft_prob = jnp.exp(draft_vals - top_draft) / sum_draft
    pick_target = jnp.take_along_axis(logits[:, :DRAFTS], draft_tokens[:, :, None], axis=2)[:, :, 0]
    pick_draft = jnp.take_along_axis(draft_vals, draft_tokens[:, :, None], axis=2)[:, :, 0]
    log_target = pick_target - top_target[:, :DRAFTS, 0] - jnp.log(sum_target[:, :DRAFTS, 0])
    log_draft = pick_draft - top_draft[:, :, 0] - jnp.log(sum_draft[:, :, 0])
    accept = jnp.exp(jnp.minimum(log_target - log_draft, 0.0))
    position = (jnp.arange(SLOTS, dtype=jnp.int32)[None, :] == reject_pos[:, None]).astype(jnp.float32)
    target_at = lax.optimization_barrier(jnp.sum(position[:, :, None] * target, axis=1))
    draft_pad = jnp.concatenate([draft_prob, jnp.zeros((REQ, 1, V), jnp.float32)], axis=1)
    draft_at = lax.optimization_barrier(jnp.sum(position[:, :, None] * draft_pad, axis=1))
    gap_rows = jnp.maximum(target_at - draft_at, 0.0)
    residual = jnp.sqrt(V * gap_rows / lax.optimization_barrier(jnp.sum(gap_rows, axis=-1, keepdims=True)))
    return (residual, accept)
```

```python
import jax
import jax.numpy as jnp
import numpy as np
from jax import lax
from jax.sharding import Mesh
from jax.sharding import PartitionSpec as P

V = 65536
DRAFTS = 4

VOCAB_AXES = ("vz", "vx", "core")
ALL_AXES = ("row",) + VOCAB_AXES
RING_ORDER = ("core", "vx", "vz", "row")


def rms_norm(values, gain):
    return values * lax.rsqrt(jnp.mean(values * values, axis=-1, keepdims=True) + 1e-06) * gain


def tree_psum(values):
    for axis in RING_ORDER:
        values = lax.psum(values, axis)
    return values


def tree_pmax(values):
    for axis in RING_ORDER:
        values = lax.pmax(values, axis)
    return values


def body(
    tokens,
    norm_gain,
    router,
    routes,
    w_gate,
    w_up,
    w_down,
    head_gain,
    head,
    draft_logits,
    draft_tokens,
    reject_pos,
):
    vocab_count = 1
    for axis in VOCAB_AXES:
        vocab_count *= lax.axis_size(axis)
    row_count = lax.axis_size("row")
    rows_dev = tokens.shape[0]
    model_width = tokens.shape[1]
    top_k = routes.shape[1]
    experts = w_gate.shape[0] * vocab_count
    capacity = min(rows_dev, (rows_dev * top_k + experts - 1) // experts)
    local_vocab = head.shape[0]
    requests = draft_tokens.shape[0]
    slot_total = DRAFTS + 1
    offset = lax.axis_index(ALL_AXES) * local_vocab
    local_ids = draft_tokens - offset
    id_match = jnp.arange(local_vocab, dtype=jnp.int32)[None, None, :] == local_ids[:, :, None]

    draft_vals = draft_logits.astype(jnp.float32)
    top_draft = tree_pmax(jnp.max(draft_vals, axis=-1))
    draft_exp = jnp.exp(draft_vals - top_draft[:, :, None])
    sum_draft, pick_d = tree_psum(
        (jnp.sum(draft_exp, axis=-1), jnp.sum(jnp.where(id_match, draft_vals, 0.0), axis=-1))
    )

    resid_in = tokens.astype(jnp.float32)
    normed = rms_norm(resid_in, norm_gain).astype(jnp.bfloat16)
    scores = jax.nn.sigmoid(jnp.dot(normed, router, preferred_element_type=jnp.float32))
    member = routes[:, :, None] == jnp.arange(experts, dtype=jnp.int32)[None, None, :]
    chosen = jnp.any(member, axis=1)
    chosen_int = chosen.astype(jnp.int32)
    picked = chosen.astype(jnp.float32) * scores
    weights = 2.5 * picked / jnp.sum(picked, axis=1, keepdims=True)
    earlier = jnp.cumsum(chosen_int, axis=0) - chosen_int
    slot_ids = jnp.arange(capacity, dtype=jnp.int32)[None, :, None]
    selector = ((earlier.T[:, None, :] == slot_ids) & chosen.T[:, None, :]).astype(jnp.float32)
    send_buffer = jnp.einsum(
        "esr,rd->sed", selector.astype(jnp.bfloat16), normed, preferred_element_type=jnp.float32
    ).astype(jnp.bfloat16)
    gate_w = w_gate[0]
    up_w = w_up[0]
    down_w = w_down[0]
    received = lax.all_to_all(send_buffer, VOCAB_AXES, split_axis=1, concat_axis=1, tiled=True)
    shard_piece = lax.all_gather(received, "row", axis=1, tiled=True)
    flat_rows = shard_piece.reshape(-1, model_width)
    gate_out = jnp.dot(flat_rows, gate_w, preferred_element_type=jnp.float32)
    up_out = jnp.dot(flat_rows, up_w, preferred_element_type=jnp.float32)
    hidden = (jax.nn.silu(gate_out) * up_out).astype(jnp.bfloat16)
    down_out = jnp.dot(hidden, down_w, preferred_element_type=jnp.float32).astype(jnp.bfloat16)
    summed = lax.psum_scatter(
        down_out.reshape(shard_piece.shape),
        "row",
        scatter_dimension=1,
        tiled=True,
    )
    returned = lax.all_to_all(summed, VOCAB_AXES, split_axis=1, concat_axis=1, tiled=True)
    combine = selector * weights.T[:, None, :]
    moe_sum = jnp.einsum(
        "esr,sed->rd", combine, returned.astype(jnp.float32), precision=lax.Precision.HIGHEST
    )
    mixed_rows = resid_in + moe_sum
    final_normed = rms_norm(mixed_rows, head_gain).astype(jnp.bfloat16)
    gathered = lax.all_gather(final_normed, ALL_AXES, axis=0, tiled=False)
    logits = jnp.einsum("gtd,wd->gtw", gathered, head, preferred_element_type=jnp.float32)
    target_logits = logits.reshape(requests, slot_total, local_vocab)
    pick_target = jnp.sum(jnp.where(id_match, target_logits[:, :DRAFTS], 0.0), axis=-1)
    top_target = tree_pmax(jnp.max(target_logits, axis=-1))
    target_exp = jnp.exp(target_logits - top_target[:, :, None])
    sum_target, pick_t = tree_psum((jnp.sum(target_exp, axis=-1), pick_target))
    target = target_exp / sum_target[:, :, None]
    draft_prob = draft_exp / sum_draft[:, :, None]
    log_target = pick_t - top_target[:, :DRAFTS] - jnp.log(sum_target[:, :DRAFTS])
    log_draft = pick_d - top_draft - jnp.log(sum_draft)
    accept = jnp.exp(jnp.minimum(log_target - log_draft, 0.0))
    position = (jnp.arange(slot_total, dtype=jnp.int32)[None, :] == reject_pos[:, None]).astype(
        jnp.float32
    )
    target_at = jnp.sum(position[:, :, None] * target, axis=1)
    draft_at = jnp.sum(position[:, :DRAFTS, None] * draft_prob, axis=1)
    gap_rows = jnp.maximum(target_at - draft_at, 0.0)
    gap_total = tree_psum(jnp.sum(gap_rows, axis=-1))
    residual = jnp.sqrt(V * gap_rows / gap_total[:, None])
    return (residual, accept)


def solution(mesh):
    row_size, vocab_size = mesh.devices.shape
    split = (row_size, 4, vocab_size // 8, 2)
    fine = Mesh(np.asarray(mesh.devices).reshape(split), ALL_AXES)
    spread = ALL_AXES
    placed = (
        P(spread, None),
        P(),
        P(),
        P(spread, None),
        P(VOCAB_AXES, None, "row"),
        P(VOCAB_AXES, None, "row"),
        P(VOCAB_AXES, "row", None),
        P(),
        P(spread, None),
        P(None, None, spread),
        P(),
        P(),
    )
    return jax.shard_map(
        body,
        mesh=fine,
        in_specs=placed,
        out_specs=(P(None, spread), P()),
        check_vma=False,
    )
```

```python
import jax
import jax.numpy as jnp
import numpy as np
from jax import lax
from jax.sharding import Mesh
from jax.sharding import PartitionSpec as P

V = 65536
DRAFTS = 4

VOCAB_AXES = ("vz", "vx", "core")
ALL_AXES = ("row",) + VOCAB_AXES


def rms_norm(values, gain):
    return values * lax.rsqrt(jnp.mean(values * values, axis=-1, keepdims=True) + 1e-06) * gain


def gather_groups():
    return (("row", "vz"), ("vx", "core"))


def merged_stats(top, total, pick):
    payload = jnp.stack([top, total, pick])
    for axes in gather_groups():
        every = lax.all_gather(payload, axes, axis=0, tiled=False)
        best = jnp.max(every[:, 0], axis=0)
        scaled = jnp.sum(every[:, 1] * jnp.exp(every[:, 0] - best[None]), axis=0)
        payload = jnp.stack([best, scaled, jnp.sum(every[:, 2], axis=0)])
    return payload[0], payload[1], payload[2]


def gathered_sum(values):
    for axes in gather_groups():
        values = jnp.sum(lax.all_gather(values, axes, axis=0, tiled=False), axis=0)
    return values


def row_reduce_scatter(parts):
    groups = parts.shape[1]
    me = lax.axis_index("row")
    total = lax.dynamic_index_in_dim(parts, me, axis=1, keepdims=False).astype(jnp.float32)
    for shift in range(1, groups):
        chunk = lax.dynamic_index_in_dim(parts, (me + shift) % groups, axis=1, keepdims=False)
        pairs = [(i, (i + shift) % groups) for i in range(groups)]
        total = total + lax.ppermute(chunk, "row", pairs).astype(jnp.float32)
    return total.astype(jnp.bfloat16)


def body(
    tokens,
    norm_gain,
    router,
    routes,
    w_gate,
    w_up,
    w_down,
    head_gain,
    head,
    draft_logits,
    draft_tokens,
    reject_pos,
):
    vocab_count = 1
    for axis in VOCAB_AXES:
        vocab_count *= lax.axis_size(axis)
    row_count = lax.axis_size("row")
    rows_dev = tokens.shape[0]
    model_width = tokens.shape[1]
    top_k = routes.shape[1]
    experts = w_gate.shape[0] * vocab_count
    capacity = min(rows_dev, (rows_dev * top_k + experts - 1) // experts)
    local_vocab = head.shape[0]
    requests = draft_tokens.shape[0]
    slot_total = DRAFTS + 1
    offset = lax.axis_index(ALL_AXES) * local_vocab
    local_ids = draft_tokens - offset
    id_match = jnp.arange(local_vocab, dtype=jnp.int32)[None, None, :] == local_ids[:, :, None]

    draft_vals = draft_logits.astype(jnp.float32)
    local_top_draft = jnp.max(draft_vals, axis=-1)
    local_sum_draft = jnp.sum(jnp.exp(draft_vals - local_top_draft[:, :, None]), axis=-1)
    local_pick_draft = jnp.sum(jnp.where(id_match, draft_vals, 0.0), axis=-1)

    resid_in = tokens.astype(jnp.float32)
    normed = rms_norm(resid_in, norm_gain).astype(jnp.bfloat16)
    scores = jax.nn.sigmoid(jnp.dot(normed, router, preferred_element_type=jnp.float32))
    member = routes[:, :, None] == jnp.arange(experts, dtype=jnp.int32)[None, None, :]
    chosen = jnp.any(member, axis=1)
    chosen_int = chosen.astype(jnp.int32)
    picked = chosen.astype(jnp.float32) * scores
    weights = 2.5 * picked / jnp.sum(picked, axis=1, keepdims=True)
    earlier = jnp.cumsum(chosen_int, axis=0) - chosen_int
    slot_ids = jnp.arange(capacity, dtype=jnp.int32)[None, :, None]
    selector = ((earlier.T[:, None, :] == slot_ids) & chosen.T[:, None, :]).astype(jnp.float32)
    send_buffer = jnp.einsum(
        "esr,rd->sed", selector.astype(jnp.bfloat16), normed, preferred_element_type=jnp.float32
    ).astype(jnp.bfloat16)
    gate_w = w_gate[0]
    up_w = w_up[0]
    down_w = w_down[0]
    received = lax.all_to_all(send_buffer, VOCAB_AXES, split_axis=1, concat_axis=1, tiled=True)
    shard_piece = lax.all_gather(received, "row", axis=1, tiled=True)
    flat_rows = shard_piece.reshape(-1, model_width)
    gate_out = jnp.dot(flat_rows, gate_w, preferred_element_type=jnp.float32)
    up_out = jnp.dot(flat_rows, up_w, preferred_element_type=jnp.float32)
    hidden = (jax.nn.silu(gate_out) * up_out).astype(jnp.bfloat16)
    down_out = jnp.dot(hidden, down_w, preferred_element_type=jnp.float32).astype(jnp.bfloat16)
    summed = row_reduce_scatter(
        down_out.reshape(capacity, row_count, -1, model_width)
    )
    returned = lax.all_to_all(summed, VOCAB_AXES, split_axis=1, concat_axis=1, tiled=True)
    combine = selector * weights.T[:, None, :]
    moe_sum = jnp.einsum(
        "esr,sed->rd", combine, returned.astype(jnp.float32), precision=lax.Precision.HIGHEST
    )
    mixed_rows = resid_in + moe_sum
    final_normed = rms_norm(mixed_rows, head_gain).astype(jnp.bfloat16)
    gathered = lax.all_gather(final_normed, ALL_AXES, axis=0, tiled=False)
    logits = jnp.einsum("gtd,wd->gtw", gathered, head, preferred_element_type=jnp.float32)
    target_logits = logits.reshape(requests, slot_total, local_vocab)
    pick_target = jnp.sum(jnp.where(id_match, target_logits[:, :DRAFTS], 0.0), axis=-1)
    local_top_target = jnp.max(target_logits, axis=-1)
    local_sum_target = jnp.sum(jnp.exp(target_logits - local_top_target[:, :, None]), axis=-1)
    pick_pad = jnp.concatenate([pick_target, jnp.zeros((requests, 1), jnp.float32)], axis=1)
    tops, sums, picks = merged_stats(
        jnp.concatenate([local_top_target, local_top_draft], axis=1),
        jnp.concatenate([local_sum_target, local_sum_draft], axis=1),
        jnp.concatenate([pick_pad, local_pick_draft], axis=1),
    )
    top_target, top_draft = tops[:, :slot_total], tops[:, slot_total:]
    sum_target, sum_draft = sums[:, :slot_total], sums[:, slot_total:]
    pick_t, pick_d = picks[:, :DRAFTS], picks[:, slot_total:]
    target_exp = jnp.exp(target_logits - top_target[:, :, None])
    draft_exp = jnp.exp(draft_vals - top_draft[:, :, None])
    target = target_exp / sum_target[:, :, None]
    draft_prob = draft_exp / sum_draft[:, :, None]
    log_target = pick_t - top_target[:, :DRAFTS] - jnp.log(sum_target[:, :DRAFTS])
    log_draft = pick_d - top_draft - jnp.log(sum_draft)
    accept = jnp.exp(jnp.minimum(log_target - log_draft, 0.0))
    position = (jnp.arange(slot_total, dtype=jnp.int32)[None, :] == reject_pos[:, None]).astype(
        jnp.float32
    )
    target_at = jnp.sum(position[:, :, None] * target, axis=1)
    draft_at = jnp.sum(position[:, :DRAFTS, None] * draft_prob, axis=1)
    gap_rows = jnp.maximum(target_at - draft_at, 0.0)
    gap_total = gathered_sum(jnp.sum(gap_rows, axis=-1))
    residual = jnp.sqrt(V * gap_rows / gap_total[:, None])
    return (residual, accept)


def solution(mesh):
    row_size, vocab_size = mesh.devices.shape
    split = (row_size, 4, vocab_size // 8, 2)
    fine = Mesh(np.asarray(mesh.devices).reshape(split), ALL_AXES)
    spread = ALL_AXES
    placed = (
        P(spread, None),
        P(),
        P(),
        P(spread, None),
        P(VOCAB_AXES, None, "row"),
        P(VOCAB_AXES, None, "row"),
        P(VOCAB_AXES, "row", None),
        P(),
        P(spread, None),
        P(None, None, spread),
        P(),
        P(),
    )
    return jax.shard_map(
        body,
        mesh=fine,
        in_specs=placed,
        out_specs=(P(None, spread), P()),
        check_vma=False,
    )
```

```python
import jax
import jax.numpy as jnp
import numpy as np
from jax import lax
from jax.sharding import Mesh
from jax.sharding import PartitionSpec as P

V = 65536
DRAFTS = 4

VOCAB_AXES = ("vz", "vx", "core")
ALL_AXES = ("row",) + VOCAB_AXES


def rms_norm(values, gain):
    return values * lax.rsqrt(jnp.mean(values * values, axis=-1, keepdims=True) + 1e-06) * gain


def gather_groups():
    return (("row", "vz"), ("vx", "core"))


def merged_stats(top, total, pick):
    payload = jnp.stack([top, total, pick])
    for axes in gather_groups():
        every = lax.all_gather(payload, axes, axis=0, tiled=False)
        best = jnp.max(every[:, 0], axis=0)
        scaled = jnp.sum(every[:, 1] * jnp.exp(every[:, 0] - best[None]), axis=0)
        payload = jnp.stack([best, scaled, jnp.sum(every[:, 2], axis=0)])
    return payload[0], payload[1], payload[2]


def gathered_sum(values):
    for axes in gather_groups():
        values = jnp.sum(lax.all_gather(values, axes, axis=0, tiled=False), axis=0)
    return values


def row_reduce_scatter(parts):
    groups = parts.shape[1]
    me = lax.axis_index("row")
    total = lax.dynamic_index_in_dim(parts, me, axis=1, keepdims=False).astype(jnp.float32)
    for shift in range(1, groups):
        chunk = lax.dynamic_index_in_dim(parts, (me + shift) % groups, axis=1, keepdims=False)
        pairs = [(i, (i + shift) % groups) for i in range(groups)]
        total = total + lax.ppermute(chunk, "row", pairs).astype(jnp.float32)
    return total.astype(jnp.bfloat16)


def body(
    tokens,
    norm_gain,
    router,
    routes,
    w_gate,
    w_up,
    w_down,
    head_gain,
    head,
    draft_logits,
    draft_tokens,
    reject_pos,
):
    vocab_count = 1
    for axis in VOCAB_AXES:
        vocab_count *= lax.axis_size(axis)
    row_count = lax.axis_size("row")
    rows_dev = tokens.shape[0]
    model_width = tokens.shape[1]
    top_k = routes.shape[1]
    experts = w_gate.shape[0] * vocab_count
    capacity = min(rows_dev, (rows_dev * top_k + experts - 1) // experts)
    local_vocab = head.shape[0]
    requests = draft_tokens.shape[0]
    slot_total = DRAFTS + 1
    offset = lax.axis_index(ALL_AXES) * local_vocab
    local_ids = draft_tokens - offset
    id_match = jnp.arange(local_vocab, dtype=jnp.int32)[None, None, :] == local_ids[:, :, None]

    draft_vals = draft_logits.astype(jnp.float32)
    local_top_draft = jnp.max(draft_vals, axis=-1)
    local_sum_draft = jnp.sum(jnp.exp(draft_vals - local_top_draft[:, :, None]), axis=-1)
    local_pick_draft = jnp.sum(jnp.where(id_match, draft_vals, 0.0), axis=-1)

    resid_in = tokens.astype(jnp.float32)
    normed = rms_norm(resid_in, norm_gain).astype(jnp.bfloat16)
    scores = jax.nn.sigmoid(jnp.dot(normed, router, preferred_element_type=jnp.float32))
    member = routes[:, :, None] == jnp.arange(experts, dtype=jnp.int32)[None, None, :]
    chosen = jnp.any(member, axis=1)
    chosen_int = chosen.astype(jnp.int32)
    picked = chosen.astype(jnp.float32) * scores
    weights = 2.5 * picked / jnp.sum(picked, axis=1, keepdims=True)
    earlier = jnp.cumsum(chosen_int, axis=0) - chosen_int
    slot_ids = jnp.arange(capacity, dtype=jnp.int32)[None, :, None]
    selector = ((earlier.T[:, None, :] == slot_ids) & chosen.T[:, None, :]).astype(jnp.float32)
    send_buffer = jnp.einsum(
        "esr,rd->sed", selector.astype(jnp.bfloat16), normed, preferred_element_type=jnp.float32
    ).astype(jnp.bfloat16)
    gate_w = w_gate[0]
    up_w = w_up[0]
    down_w = w_down[0]
    received = lax.all_to_all(send_buffer, VOCAB_AXES, split_axis=1, concat_axis=1, tiled=True)
    shard_piece = lax.all_gather(received, "row", axis=1, tiled=True)
    flat_rows = shard_piece.reshape(-1, model_width)
    gate_out = jnp.dot(flat_rows, gate_w, preferred_element_type=jnp.float32)
    up_out = jnp.dot(flat_rows, up_w, preferred_element_type=jnp.float32)
    hidden = (jax.nn.silu(gate_out) * up_out).astype(jnp.bfloat16)
    down_out = jnp.dot(hidden, down_w, preferred_element_type=jnp.float32).astype(jnp.bfloat16)
    summed = row_reduce_scatter(
        down_out.reshape(capacity, row_count, -1, model_width)
    )
    returned = lax.all_to_all(summed, VOCAB_AXES, split_axis=1, concat_axis=1, tiled=True)
    combine = selector * weights.T[:, None, :]
    moe_sum = jnp.einsum(
        "esr,sed->rd", combine, returned.astype(jnp.float32), precision=lax.Precision.HIGHEST
    )
    mixed_rows = resid_in + moe_sum
    final_normed = rms_norm(mixed_rows, head_gain).astype(jnp.bfloat16)
    gathered = lax.all_gather(final_normed, ALL_AXES, axis=1, tiled=False)
    logits = jnp.einsum("tgd,wd->tgw", gathered, head, preferred_element_type=jnp.float32)
    halves = rows_dev // slot_total
    target_logits = logits.reshape(halves, slot_total, -1, local_vocab)

    def to_requests(values):
        return jnp.transpose(values, (2, 0, 1)).reshape(requests, slot_total)

    def from_requests(values):
        return jnp.transpose(values.reshape(-1, halves, slot_total), (1, 2, 0))

    ids_t = from_requests(
        jnp.concatenate([local_ids, jnp.full((requests, 1), -1, jnp.int32)], axis=1)
    )
    id_match_t = jnp.arange(local_vocab, dtype=jnp.int32) == ids_t[..., None]
    pick_target = to_requests(jnp.sum(jnp.where(id_match_t, target_logits, 0.0), axis=-1))
    local_top_t = jnp.max(target_logits, axis=-1)
    local_sum_target = to_requests(
        jnp.sum(jnp.exp(target_logits - local_top_t[..., None]), axis=-1)
    )
    local_top_target = to_requests(local_top_t)
    tops, sums, picks = merged_stats(
        jnp.concatenate([local_top_target, local_top_draft], axis=1),
        jnp.concatenate([local_sum_target, local_sum_draft], axis=1),
        jnp.concatenate([pick_target, local_pick_draft], axis=1),
    )
    top_target, top_draft = tops[:, :slot_total], tops[:, slot_total:]
    sum_target, sum_draft = sums[:, :slot_total], sums[:, slot_total:]
    pick_t, pick_d = picks[:, :DRAFTS], picks[:, slot_total:]
    draft_exp = jnp.exp(draft_vals - top_draft[:, :, None])
    draft_prob = draft_exp / sum_draft[:, :, None]
    log_target = pick_t - top_target[:, :DRAFTS] - jnp.log(sum_target[:, :DRAFTS])
    log_draft = pick_d - top_draft - jnp.log(sum_draft)
    accept = jnp.exp(jnp.minimum(log_target - log_draft, 0.0))
    position = (jnp.arange(slot_total, dtype=jnp.int32)[None, :] == reject_pos[:, None]).astype(
        jnp.float32
    )
    weight_t = from_requests(position / sum_target)
    target_at = jnp.sum(
        weight_t[..., None] * jnp.exp(target_logits - from_requests(top_target)[..., None]), axis=1
    )
    target_at = jnp.transpose(target_at, (1, 0, 2)).reshape(requests, local_vocab)
    draft_at = jnp.sum(position[:, :DRAFTS, None] * draft_prob, axis=1)
    gap_rows = jnp.maximum(target_at - draft_at, 0.0)
    gap_total = gathered_sum(jnp.sum(gap_rows, axis=-1))
    residual = jnp.sqrt(V * gap_rows / gap_total[:, None])
    return (residual, accept)


def solution(mesh):
    row_size, vocab_size = mesh.devices.shape
    split = (row_size, 4, vocab_size // 8, 2)
    fine = Mesh(np.asarray(mesh.devices).reshape(split), ALL_AXES)
    spread = ALL_AXES
    placed = (
        P(spread, None),
        P(),
        P(),
        P(spread, None),
        P(VOCAB_AXES, None, "row"),
        P(VOCAB_AXES, None, "row"),
        P(VOCAB_AXES, "row", None),
        P(),
        P(spread, None),
        P(None, None, spread),
        P(),
        P(),
    )
    return jax.shard_map(
        body,
        mesh=fine,
        in_specs=placed,
        out_specs=(P(None, spread), P()),
        check_vma=False,
    )
```

```python
import jax
import jax.numpy as jnp
import numpy as np
from jax import lax
from jax.sharding import Mesh
from jax.sharding import PartitionSpec as P

V = 65536
DRAFTS = 4

VOCAB_AXES = ("vz", "vx", "core")
ALL_AXES = ("row",) + VOCAB_AXES


def rms_norm(values, gain):
    return values * lax.rsqrt(jnp.mean(values * values, axis=-1, keepdims=True) + 1e-06) * gain


def gather_groups():
    return (("row", "vz"), ("vx", "core"))


def merged_stats(top, total, pick):
    payload = jnp.stack([top, total, pick])
    for axes in gather_groups():
        every = lax.all_gather(payload, axes, axis=0, tiled=False)
        best = jnp.max(every[:, 0], axis=0)
        scaled = jnp.sum(every[:, 1] * jnp.exp(every[:, 0] - best[None]), axis=0)
        payload = jnp.stack([best, scaled, jnp.sum(every[:, 2], axis=0)])
    return payload[0], payload[1], payload[2]


def gathered_sum(values):
    for axes in gather_groups():
        values = jnp.sum(lax.all_gather(values, axes, axis=0, tiled=False), axis=0)
    return values


def row_reduce_scatter(parts):
    groups = parts.shape[1]
    me = lax.axis_index("row")
    total = lax.dynamic_index_in_dim(parts, me, axis=1, keepdims=False).astype(jnp.float32)
    for shift in range(1, groups):
        chunk = lax.dynamic_index_in_dim(parts, (me + shift) % groups, axis=1, keepdims=False)
        pairs = [(i, (i + shift) % groups) for i in range(groups)]
        total = total + lax.ppermute(chunk, "row", pairs).astype(jnp.float32)
    return total.astype(jnp.bfloat16)


def body(
    tokens,
    norm_gain,
    router,
    routes,
    w_gate,
    w_up,
    w_down,
    head_gain,
    head,
    draft_logits,
    draft_tokens,
    reject_pos,
):
    vocab_count = 1
    for axis in VOCAB_AXES:
        vocab_count *= lax.axis_size(axis)
    row_count = lax.axis_size("row")
    rows_dev = tokens.shape[0]
    model_width = tokens.shape[1]
    top_k = routes.shape[1]
    experts = w_gate.shape[0] * vocab_count
    capacity = min(rows_dev, (rows_dev * top_k + experts - 1) // experts)
    local_vocab = head.shape[0]
    requests = draft_tokens.shape[0]
    slot_total = DRAFTS + 1
    offset = lax.axis_index(ALL_AXES) * local_vocab
    local_ids = draft_tokens - offset
    id_match = jnp.arange(local_vocab, dtype=jnp.int32)[None, None, :] == local_ids[:, :, None]

    draft_vals = draft_logits.astype(jnp.float32)
    local_top_draft = jnp.max(draft_vals, axis=-1)
    local_sum_draft = jnp.sum(jnp.exp(draft_vals - local_top_draft[:, :, None]), axis=-1)
    local_pick_draft = jnp.sum(jnp.where(id_match, draft_vals, 0.0), axis=-1)

    resid_in = tokens.astype(jnp.float32)
    normed = rms_norm(resid_in, norm_gain).astype(jnp.bfloat16)
    scores = jax.nn.sigmoid(jnp.dot(normed, router, preferred_element_type=jnp.float32))
    member = routes[:, :, None] == jnp.arange(experts, dtype=jnp.int32)[None, None, :]
    chosen = jnp.any(member, axis=1)
    chosen_int = chosen.astype(jnp.int32)
    picked = chosen.astype(jnp.float32) * scores
    weights = 2.5 * picked / jnp.sum(picked, axis=1, keepdims=True)
    earlier = jnp.cumsum(chosen_int, axis=0) - chosen_int
    slot_ids = jnp.arange(capacity, dtype=jnp.int32)[None, :, None]
    selector = ((earlier.T[:, None, :] == slot_ids) & chosen.T[:, None, :]).astype(jnp.float32)
    send_buffer = jnp.einsum(
        "esr,rd->sed", selector.astype(jnp.bfloat16), normed, preferred_element_type=jnp.float32
    ).astype(jnp.bfloat16)
    gate_w = w_gate[0]
    up_w = w_up[0]
    down_w = w_down[0]
    received = lax.all_to_all(send_buffer, VOCAB_AXES, split_axis=1, concat_axis=1, tiled=True)
    shard_piece = lax.all_gather(received, "row", axis=1, tiled=True)
    flat_rows = shard_piece.reshape(-1, model_width)
    gate_out = jnp.dot(flat_rows, gate_w, preferred_element_type=jnp.float32)
    up_out = jnp.dot(flat_rows, up_w, preferred_element_type=jnp.float32)
    hidden = (jax.nn.silu(gate_out) * up_out).astype(jnp.bfloat16)
    down_out = jnp.dot(hidden, down_w, preferred_element_type=jnp.float32).astype(jnp.bfloat16)
    summed = row_reduce_scatter(
        down_out.reshape(capacity, row_count, -1, model_width)
    )
    returned = lax.all_to_all(summed, VOCAB_AXES, split_axis=1, concat_axis=1, tiled=True)
    combine = selector * weights.T[:, None, :]
    moe_sum = jnp.einsum(
        "esr,sed->rd", combine, returned.astype(jnp.float32), precision=lax.Precision.HIGHEST
    )
    mixed_rows = resid_in + moe_sum
    final_normed = rms_norm(mixed_rows, head_gain).astype(jnp.bfloat16)
    halves = rows_dev // slot_total
    parts = []
    for half in range(halves):
        piece = final_normed[half * slot_total:(half + 1) * slot_total]
        gathered = lax.all_gather(piece, ALL_AXES, axis=1, tiled=False)
        parts.append(jnp.einsum("tgd,wd->tgw", gathered, head, preferred_element_type=jnp.float32))
    target_logits = jnp.stack(parts)

    def to_requests(values):
        return jnp.transpose(values, (2, 0, 1)).reshape(requests, slot_total)

    def from_requests(values):
        return jnp.transpose(values.reshape(-1, halves, slot_total), (1, 2, 0))

    ids_t = from_requests(
        jnp.concatenate([local_ids, jnp.full((requests, 1), -1, jnp.int32)], axis=1)
    )
    id_match_t = jnp.arange(local_vocab, dtype=jnp.int32) == ids_t[..., None]
    pick_target = to_requests(jnp.sum(jnp.where(id_match_t, target_logits, 0.0), axis=-1))
    local_top_t = jnp.max(target_logits, axis=-1)
    local_sum_target = to_requests(
        jnp.sum(jnp.exp(target_logits - local_top_t[..., None]), axis=-1)
    )
    local_top_target = to_requests(local_top_t)
    tops, sums, picks = merged_stats(
        jnp.concatenate([local_top_target, local_top_draft], axis=1),
        jnp.concatenate([local_sum_target, local_sum_draft], axis=1),
        jnp.concatenate([pick_target, local_pick_draft], axis=1),
    )
    top_target, top_draft = tops[:, :slot_total], tops[:, slot_total:]
    sum_target, sum_draft = sums[:, :slot_total], sums[:, slot_total:]
    pick_t, pick_d = picks[:, :DRAFTS], picks[:, slot_total:]
    draft_exp = jnp.exp(draft_vals - top_draft[:, :, None])
    draft_prob = draft_exp / sum_draft[:, :, None]
    log_target = pick_t - top_target[:, :DRAFTS] - jnp.log(sum_target[:, :DRAFTS])
    log_draft = pick_d - top_draft - jnp.log(sum_draft)
    accept = jnp.exp(jnp.minimum(log_target - log_draft, 0.0))
    position = (jnp.arange(slot_total, dtype=jnp.int32)[None, :] == reject_pos[:, None]).astype(
        jnp.float32
    )
    weight_t = from_requests(position / sum_target)
    target_at = jnp.sum(
        weight_t[..., None] * jnp.exp(target_logits - from_requests(top_target)[..., None]), axis=1
    )
    target_at = jnp.transpose(target_at, (1, 0, 2)).reshape(requests, local_vocab)
    draft_at = jnp.sum(position[:, :DRAFTS, None] * draft_prob, axis=1)
    gap_rows = jnp.maximum(target_at - draft_at, 0.0)
    gap_total = gathered_sum(jnp.sum(gap_rows, axis=-1))
    residual = jnp.sqrt(V * gap_rows / gap_total[:, None])
    return (residual, accept)


def solution(mesh):
    row_size, vocab_size = mesh.devices.shape
    split = (row_size, 4, vocab_size // 8, 2)
    fine = Mesh(np.asarray(mesh.devices).reshape(split), ALL_AXES)
    spread = ALL_AXES
    placed = (
        P(spread, None),
        P(),
        P(),
        P(spread, None),
        P(VOCAB_AXES, None, "row"),
        P(VOCAB_AXES, None, "row"),
        P(VOCAB_AXES, "row", None),
        P(),
        P(spread, None),
        P(None, None, spread),
        P(),
        P(),
    )
    return jax.shard_map(
        body,
        mesh=fine,
        in_specs=placed,
        out_specs=(P(None, spread), P()),
        check_vma=False,
    )
```

```python
import jax
import jax.numpy as jnp
import numpy as np
from jax import lax
from jax.sharding import Mesh
from jax.sharding import PartitionSpec as P

V = 65536
DRAFTS = 4

VOCAB_AXES = ("vz", "vx", "core")
ALL_AXES = ("row",) + VOCAB_AXES


def rms_norm(values, gain):
    return values * lax.rsqrt(jnp.mean(values * values, axis=-1, keepdims=True) + 1e-06) * gain


def gather_groups():
    return (("row", "vz"), ("vx", "core"))


def merged_stats(top, total, pick):
    payload = jnp.stack([top, total, pick])
    for axes in gather_groups():
        every = lax.all_gather(payload, axes, axis=0, tiled=False)
        best = jnp.max(every[:, 0], axis=0)
        scaled = jnp.sum(every[:, 1] * jnp.exp(every[:, 0] - best[None]), axis=0)
        payload = jnp.stack([best, scaled, jnp.sum(every[:, 2], axis=0)])
    return payload[0], payload[1], payload[2]


def gathered_sum(values):
    for axes in gather_groups():
        values = jnp.sum(lax.all_gather(values, axes, axis=0, tiled=False), axis=0)
    return values


def row_reduce_scatter(parts):
    groups = parts.shape[1]
    me = lax.axis_index("row")
    total = lax.dynamic_index_in_dim(parts, me, axis=1, keepdims=False).astype(jnp.float32)
    for shift in range(1, groups):
        chunk = lax.dynamic_index_in_dim(parts, (me + shift) % groups, axis=1, keepdims=False)
        pairs = [(i, (i + shift) % groups) for i in range(groups)]
        total = total + lax.ppermute(chunk, "row", pairs).astype(jnp.float32)
    return total.astype(jnp.bfloat16)


def body(
    tokens,
    norm_gain,
    router,
    routes,
    w_gate,
    w_up,
    w_down,
    head_gain,
    head,
    draft_logits,
    draft_tokens,
    reject_pos,
):
    vocab_count = 1
    for axis in VOCAB_AXES:
        vocab_count *= lax.axis_size(axis)
    row_count = lax.axis_size("row")
    rows_dev = tokens.shape[0]
    model_width = tokens.shape[1]
    top_k = routes.shape[1]
    experts = w_gate.shape[0] * vocab_count
    capacity = min(rows_dev, (rows_dev * top_k + experts - 1) // experts)
    local_vocab = head.shape[0]
    requests = draft_tokens.shape[0]
    slot_total = DRAFTS + 1
    offset = lax.axis_index(ALL_AXES) * local_vocab
    local_ids = draft_tokens - offset
    id_match = jnp.arange(local_vocab, dtype=jnp.int32)[None, None, :] == local_ids[:, :, None]

    draft_vals = draft_logits.astype(jnp.float32)
    local_top_draft = jnp.max(draft_vals, axis=-1)
    local_sum_draft = jnp.sum(jnp.exp(draft_vals - local_top_draft[:, :, None]), axis=-1)
    local_pick_draft = jnp.sum(jnp.where(id_match, draft_vals, 0.0), axis=-1)

    resid_in = tokens.astype(jnp.float32)
    normed = rms_norm(resid_in, norm_gain).astype(jnp.bfloat16)
    scores = jax.nn.sigmoid(jnp.dot(normed, router, preferred_element_type=jnp.float32))
    member = routes[:, :, None] == jnp.arange(experts, dtype=jnp.int32)[None, None, :]
    chosen = jnp.any(member, axis=1)
    chosen_int = chosen.astype(jnp.int32)
    picked = chosen.astype(jnp.float32) * scores
    weights = 2.5 * picked / jnp.sum(picked, axis=1, keepdims=True)
    earlier = jnp.cumsum(chosen_int, axis=0) - chosen_int
    slot_ids = jnp.arange(capacity, dtype=jnp.int32)[None, :, None]
    selector = ((earlier.T[:, None, :] == slot_ids) & chosen.T[:, None, :]).astype(jnp.float32)
    send_buffer = jnp.einsum(
        "esr,rd->sed", selector.astype(jnp.bfloat16), normed, preferred_element_type=jnp.float32
    ).astype(jnp.bfloat16)
    gate_w = w_gate[0]
    up_w = w_up[0]
    down_w = w_down[0]
    received = lax.all_to_all(send_buffer, VOCAB_AXES, split_axis=1, concat_axis=1, tiled=True)
    shard_piece = lax.all_gather(received, "row", axis=1, tiled=True)
    flat_rows = shard_piece.reshape(-1, model_width)
    gate_out = jnp.dot(flat_rows, gate_w, preferred_element_type=jnp.float32)
    up_out = jnp.dot(flat_rows, up_w, preferred_element_type=jnp.float32)
    hidden = (jax.nn.silu(gate_out) * up_out).astype(jnp.bfloat16)
    down_out = jnp.dot(hidden, down_w, preferred_element_type=jnp.float32).astype(jnp.bfloat16)
    summed = row_reduce_scatter(
        down_out.reshape(capacity, row_count, -1, model_width)
    )
    returned = lax.all_to_all(summed, VOCAB_AXES, split_axis=1, concat_axis=1, tiled=True)
    combine = selector * weights.T[:, None, :]
    moe_sum = jnp.einsum(
        "esr,sed->rd", combine, returned.astype(jnp.float32), precision=lax.Precision.HIGHEST
    )
    mixed_rows = resid_in + moe_sum
    final_normed = rms_norm(mixed_rows, head_gain).astype(jnp.bfloat16)
    halves = rows_dev // slot_total
    gathered = lax.all_gather(final_normed, ALL_AXES, axis=1, tiled=False)
    target_logits = jnp.stack(
        [
            jnp.einsum(
                "tgd,wd->tgw",
                gathered[half * slot_total:(half + 1) * slot_total],
                head,
                preferred_element_type=jnp.float32,
            )
            for half in range(halves)
        ]
    )

    def to_requests(values):
        return jnp.transpose(values, (2, 0, 1)).reshape(requests, slot_total)

    def from_requests(values):
        return jnp.transpose(values.reshape(-1, halves, slot_total), (1, 2, 0))

    ids_t = from_requests(
        jnp.concatenate([local_ids, jnp.full((requests, 1), -1, jnp.int32)], axis=1)
    )
    id_match_t = jnp.arange(local_vocab, dtype=jnp.int32) == ids_t[..., None]
    pick_target = to_requests(jnp.sum(jnp.where(id_match_t, target_logits, 0.0), axis=-1))
    local_top_t = jnp.max(target_logits, axis=-1)
    local_sum_target = to_requests(
        jnp.sum(jnp.exp(target_logits - local_top_t[..., None]), axis=-1)
    )
    local_top_target = to_requests(local_top_t)
    tops, sums, picks = merged_stats(
        jnp.concatenate([local_top_target, local_top_draft], axis=1),
        jnp.concatenate([local_sum_target, local_sum_draft], axis=1),
        jnp.concatenate([pick_target, local_pick_draft], axis=1),
    )
    top_target, top_draft = tops[:, :slot_total], tops[:, slot_total:]
    sum_target, sum_draft = sums[:, :slot_total], sums[:, slot_total:]
    pick_t, pick_d = picks[:, :DRAFTS], picks[:, slot_total:]
    draft_exp = jnp.exp(draft_vals - top_draft[:, :, None])
    draft_prob = draft_exp / sum_draft[:, :, None]
    log_target = pick_t - top_target[:, :DRAFTS] - jnp.log(sum_target[:, :DRAFTS])
    log_draft = pick_d - top_draft - jnp.log(sum_draft)
    accept = jnp.exp(jnp.minimum(log_target - log_draft, 0.0))
    position = (jnp.arange(slot_total, dtype=jnp.int32)[None, :] == reject_pos[:, None]).astype(
        jnp.float32
    )
    weight_t = from_requests(position / sum_target)
    target_at = jnp.sum(
        weight_t[..., None] * jnp.exp(target_logits - from_requests(top_target)[..., None]), axis=1
    )
    target_at = jnp.transpose(target_at, (1, 0, 2)).reshape(requests, local_vocab)
    draft_at = jnp.sum(position[:, :DRAFTS, None] * draft_prob, axis=1)
    gap_rows = jnp.maximum(target_at - draft_at, 0.0)
    gap_total = gathered_sum(jnp.sum(gap_rows, axis=-1))
    residual = jnp.sqrt(V * gap_rows / gap_total[:, None])
    return (residual, accept)


def solution(mesh):
    row_size, vocab_size = mesh.devices.shape
    split = (row_size, 4, vocab_size // 8, 2)
    fine = Mesh(np.asarray(mesh.devices).reshape(split), ALL_AXES)
    spread = ALL_AXES
    placed = (
        P(spread, None),
        P(),
        P(),
        P(spread, None),
        P(VOCAB_AXES, None, "row"),
        P(VOCAB_AXES, None, "row"),
        P(VOCAB_AXES, "row", None),
        P(),
        P(spread, None),
        P(None, None, spread),
        P(),
        P(),
    )
    return jax.shard_map(
        body,
        mesh=fine,
        in_specs=placed,
        out_specs=(P(None, spread), P()),
        check_vma=False,
    )
```

```python
import jax
import jax.numpy as jnp
import numpy as np
from jax import lax
from jax.sharding import Mesh
from jax.sharding import PartitionSpec as P

V = 65536
DRAFTS = 4

VOCAB_AXES = ("vz", "vx", "core")
ALL_AXES = ("row",) + VOCAB_AXES


def rms_norm(values, gain):
    return values * lax.rsqrt(jnp.mean(values * values, axis=-1, keepdims=True) + 1e-06) * gain


def gather_groups():
    return (("row", "vz"), ("vx", "core"))


def merged_stats(top, total, pick):
    payload = jnp.stack([top, total, pick])
    for axes in gather_groups():
        every = lax.all_gather(payload, axes, axis=0, tiled=False)
        best = jnp.max(every[:, 0], axis=0)
        scaled = jnp.sum(every[:, 1] * jnp.exp(every[:, 0] - best[None]), axis=0)
        payload = jnp.stack([best, scaled, jnp.sum(every[:, 2], axis=0)])
    return payload[0], payload[1], payload[2]


def gathered_sum(values):
    for axes in gather_groups():
        values = jnp.sum(lax.all_gather(values, axes, axis=0, tiled=False), axis=0)
    return values


def row_reduce_scatter(parts):
    groups = parts.shape[1]
    me = lax.axis_index("row")
    total = lax.dynamic_index_in_dim(parts, me, axis=1, keepdims=False).astype(jnp.float32)
    for shift in range(1, groups):
        chunk = lax.dynamic_index_in_dim(parts, (me + shift) % groups, axis=1, keepdims=False)
        pairs = [(i, (i + shift) % groups) for i in range(groups)]
        total = total + lax.ppermute(chunk, "row", pairs).astype(jnp.float32)
    return total.astype(jnp.bfloat16)


def body(
    tokens,
    norm_gain,
    router,
    routes,
    w_gate,
    w_up,
    w_down,
    head_gain,
    head,
    draft_logits,
    draft_tokens,
    reject_pos,
):
    vocab_count = 1
    for axis in VOCAB_AXES:
        vocab_count *= lax.axis_size(axis)
    row_count = lax.axis_size("row")
    rows_dev = tokens.shape[0]
    model_width = tokens.shape[1]
    top_k = routes.shape[1]
    experts = w_gate.shape[0] * vocab_count
    capacity = min(rows_dev, (rows_dev * top_k + experts - 1) // experts)
    local_vocab = head.shape[0]
    requests = draft_tokens.shape[0]
    slot_total = DRAFTS + 1
    offset = lax.axis_index(ALL_AXES) * local_vocab
    local_ids = draft_tokens - offset
    id_match = jnp.arange(local_vocab, dtype=jnp.int32)[None, None, :] == local_ids[:, :, None]

    draft_vals = draft_logits.astype(jnp.float32)
    local_top_draft = jnp.max(draft_vals, axis=-1)
    local_sum_draft = jnp.sum(jnp.exp(draft_vals - local_top_draft[:, :, None]), axis=-1)
    local_pick_draft = jnp.sum(jnp.where(id_match, draft_vals, 0.0), axis=-1)

    resid_in = tokens.astype(jnp.float32)
    normed = rms_norm(resid_in, norm_gain).astype(jnp.bfloat16)
    scores = jax.nn.sigmoid(jnp.dot(normed, router, preferred_element_type=jnp.float32))
    member = routes[:, :, None] == jnp.arange(experts, dtype=jnp.int32)[None, None, :]
    chosen = jnp.any(member, axis=1)
    chosen_int = chosen.astype(jnp.int32)
    picked = chosen.astype(jnp.float32) * scores
    weights = 2.5 * picked / jnp.sum(picked, axis=1, keepdims=True)
    earlier = jnp.cumsum(chosen_int, axis=0) - chosen_int
    slot_ids = jnp.arange(capacity, dtype=jnp.int32)[None, :, None]
    selector = ((earlier.T[:, None, :] == slot_ids) & chosen.T[:, None, :]).astype(jnp.float32)
    send_buffer = jnp.einsum(
        "esr,rd->sed", selector.astype(jnp.bfloat16), normed, preferred_element_type=jnp.float32
    ).astype(jnp.bfloat16)
    gate_w = w_gate[0]
    up_w = w_up[0]
    down_w = w_down[0]
    received = lax.all_to_all(send_buffer, VOCAB_AXES, split_axis=1, concat_axis=1, tiled=True)
    shard_piece = lax.all_gather(received, "row", axis=1, tiled=True)
    flat_rows = shard_piece.reshape(-1, model_width)
    gate_out = jnp.dot(flat_rows, gate_w, preferred_element_type=jnp.float32)
    up_out = jnp.dot(flat_rows, up_w, preferred_element_type=jnp.float32)
    hidden = (jax.nn.silu(gate_out) * up_out).astype(jnp.bfloat16)
    down_out = jnp.dot(hidden, down_w, preferred_element_type=jnp.float32).astype(jnp.bfloat16)
    summed = row_reduce_scatter(
        down_out.reshape(capacity, row_count, -1, model_width)
    )
    returned = lax.all_to_all(summed, VOCAB_AXES, split_axis=1, concat_axis=1, tiled=True)
    combine = selector * weights.T[:, None, :]
    moe_sum = jnp.einsum(
        "esr,sed->rd", combine, returned.astype(jnp.float32), precision=lax.Precision.HIGHEST
    )
    mixed_rows = resid_in + moe_sum
    final_normed = rms_norm(mixed_rows, head_gain).astype(jnp.bfloat16)
    padded = -(-rows_dev // 16) * 16
    block = jnp.concatenate(
        [final_normed, jnp.zeros((padded - rows_dev, model_width), final_normed.dtype)]
    )
    gathered = lax.all_gather(block, ALL_AXES, axis=0, tiled=True)
    devices = gathered.shape[0] // padded
    logits = lax.dot_general(
        gathered, head, (((1,), (1,)), ((), ())), preferred_element_type=jnp.float32
    )
    target_logits = logits.reshape(devices, padded, local_vocab)
    halves = rows_dev // slot_total

    def to_requests(values):
        return values[:, :rows_dev].reshape(requests, slot_total)

    def from_requests(values, fill):
        grid = values.reshape(devices, rows_dev)
        return jnp.concatenate(
            [grid, jnp.full((devices, padded - rows_dev), fill, grid.dtype)], axis=1
        )

    ids_t = from_requests(
        jnp.concatenate([local_ids, jnp.full((requests, 1), -1, jnp.int32)], axis=1), -1
    )
    id_match_t = jnp.arange(local_vocab, dtype=jnp.int32) == ids_t[..., None]
    pick_target = to_requests(jnp.sum(jnp.where(id_match_t, target_logits, 0.0), axis=-1))
    local_top_t = jnp.max(target_logits, axis=-1)
    local_sum_target = to_requests(
        jnp.sum(jnp.exp(target_logits - local_top_t[..., None]), axis=-1)
    )
    local_top_target = to_requests(local_top_t)
    tops, sums, picks = merged_stats(
        jnp.concatenate([local_top_target, local_top_draft], axis=1),
        jnp.concatenate([local_sum_target, local_sum_draft], axis=1),
        jnp.concatenate([pick_target, local_pick_draft], axis=1),
    )
    top_target, top_draft = tops[:, :slot_total], tops[:, slot_total:]
    sum_target, sum_draft = sums[:, :slot_total], sums[:, slot_total:]
    pick_t, pick_d = picks[:, :DRAFTS], picks[:, slot_total:]
    draft_exp = jnp.exp(draft_vals - top_draft[:, :, None])
    draft_prob = draft_exp / sum_draft[:, :, None]
    log_target = pick_t - top_target[:, :DRAFTS] - jnp.log(sum_target[:, :DRAFTS])
    log_draft = pick_d - top_draft - jnp.log(sum_draft)
    accept = jnp.exp(jnp.minimum(log_target - log_draft, 0.0))
    position = (jnp.arange(slot_total, dtype=jnp.int32)[None, :] == reject_pos[:, None]).astype(
        jnp.float32
    )
    weight_t = from_requests(position / sum_target, 0.0)
    weighted = weight_t[..., None] * jnp.exp(
        target_logits - from_requests(top_target, 0.0)[..., None]
    )
    target_at = jnp.stack(
        [
            jnp.sum(weighted[:, half * slot_total:(half + 1) * slot_total], axis=1)
            for half in range(halves)
        ],
        axis=1,
    ).reshape(requests, local_vocab)
    draft_at = jnp.sum(position[:, :DRAFTS, None] * draft_prob, axis=1)
    gap_rows = jnp.maximum(target_at - draft_at, 0.0)
    gap_total = gathered_sum(jnp.sum(gap_rows, axis=-1))
    residual = jnp.sqrt(V * gap_rows / gap_total[:, None])
    return (residual, accept)


def solution(mesh):
    row_size, vocab_size = mesh.devices.shape
    split = (row_size, 4, vocab_size // 8, 2)
    fine = Mesh(np.asarray(mesh.devices).reshape(split), ALL_AXES)
    spread = ALL_AXES
    placed = (
        P(spread, None),
        P(),
        P(),
        P(spread, None),
        P(VOCAB_AXES, None, "row"),
        P(VOCAB_AXES, None, "row"),
        P(VOCAB_AXES, "row", None),
        P(),
        P(spread, None),
        P(None, None, spread),
        P(),
        P(),
    )
    return jax.shard_map(
        body,
        mesh=fine,
        in_specs=placed,
        out_specs=(P(None, spread), P()),
        check_vma=False,
    )
```

```python
import jax
import jax.numpy as jnp
import numpy as np
from jax import lax
from jax.sharding import Mesh
from jax.sharding import PartitionSpec as P

V = 65536
DRAFTS = 4

VOCAB_AXES = ("vz", "vx", "core")
ALL_AXES = ("row",) + VOCAB_AXES


def rms_norm(values, gain):
    return values * lax.rsqrt(jnp.mean(values * values, axis=-1, keepdims=True) + 1e-06) * gain


def gather_groups():
    return (("row", "vz"), ("vx", "core"))


def merged_stats(top, total, pick):
    payload = jnp.stack([top.T, total.T, pick.T])
    for axes in gather_groups():
        every = lax.all_gather(payload, axes, axis=0, tiled=False)
        best = jnp.max(every[:, 0], axis=0)
        scaled = jnp.sum(every[:, 1] * jnp.exp(every[:, 0] - best[None]), axis=0)
        payload = jnp.stack([best, scaled, jnp.sum(every[:, 2], axis=0)])
    return payload[0].T, payload[1].T, payload[2].T


def gathered_sum(values):
    for axes in gather_groups():
        values = jnp.sum(lax.all_gather(values, axes, axis=0, tiled=False), axis=0)
    return values


def row_reduce_scatter(parts):
    groups = parts.shape[1]
    me = lax.axis_index("row")
    total = lax.dynamic_index_in_dim(parts, me, axis=1, keepdims=False).astype(jnp.float32)
    for shift in range(1, groups):
        chunk = lax.dynamic_index_in_dim(parts, (me + shift) % groups, axis=1, keepdims=False)
        pairs = [(i, (i + shift) % groups) for i in range(groups)]
        total = total + lax.ppermute(chunk, "row", pairs).astype(jnp.float32)
    return total.astype(jnp.bfloat16)


def body(
    tokens,
    norm_gain,
    router,
    routes,
    w_gate,
    w_up,
    w_down,
    head_gain,
    head,
    draft_logits,
    draft_tokens,
    reject_pos,
):
    vocab_count = 1
    for axis in VOCAB_AXES:
        vocab_count *= lax.axis_size(axis)
    row_count = lax.axis_size("row")
    rows_dev = tokens.shape[0]
    model_width = tokens.shape[1]
    top_k = routes.shape[1]
    experts = w_gate.shape[0] * vocab_count
    capacity = min(rows_dev, (rows_dev * top_k + experts - 1) // experts)
    local_vocab = head.shape[0]
    requests = draft_tokens.shape[0]
    slot_total = DRAFTS + 1
    offset = lax.axis_index(ALL_AXES) * local_vocab
    local_ids = draft_tokens - offset
    id_match = jnp.arange(local_vocab, dtype=jnp.int32)[None, None, :] == local_ids[:, :, None]

    draft_vals = draft_logits.astype(jnp.float32)
    local_top_draft = jnp.max(draft_vals, axis=-1)
    local_sum_draft = jnp.sum(jnp.exp(draft_vals - local_top_draft[:, :, None]), axis=-1)
    local_pick_draft = jnp.sum(jnp.where(id_match, draft_vals, 0.0), axis=-1)

    resid_in = tokens.astype(jnp.float32)
    normed = rms_norm(resid_in, norm_gain).astype(jnp.bfloat16)
    scores = jax.nn.sigmoid(jnp.dot(normed, router, preferred_element_type=jnp.float32))
    member = routes[:, :, None] == jnp.arange(experts, dtype=jnp.int32)[None, None, :]
    chosen = jnp.any(member, axis=1)
    chosen_int = chosen.astype(jnp.int32)
    picked = chosen.astype(jnp.float32) * scores
    weights = 2.5 * picked / jnp.sum(picked, axis=1, keepdims=True)
    earlier = jnp.cumsum(chosen_int, axis=0) - chosen_int
    slot_ids = jnp.arange(capacity, dtype=jnp.int32)[None, :, None]
    selector = ((earlier.T[:, None, :] == slot_ids) & chosen.T[:, None, :]).astype(jnp.float32)
    send_buffer = jnp.einsum(
        "esr,rd->sed", selector.astype(jnp.bfloat16), normed, preferred_element_type=jnp.float32
    ).astype(jnp.bfloat16)
    gate_w = w_gate[0]
    up_w = w_up[0]
    down_w = w_down[0]
    received = lax.all_to_all(send_buffer, VOCAB_AXES, split_axis=1, concat_axis=1, tiled=True)
    shard_piece = lax.all_gather(received, "row", axis=1, tiled=True)
    flat_rows = shard_piece.reshape(-1, model_width)
    gate_out = jnp.dot(flat_rows, gate_w, preferred_element_type=jnp.float32)
    up_out = jnp.dot(flat_rows, up_w, preferred_element_type=jnp.float32)
    hidden = (jax.nn.silu(gate_out) * up_out).astype(jnp.bfloat16)
    down_out = jnp.dot(hidden, down_w, preferred_element_type=jnp.float32).astype(jnp.bfloat16)
    summed = row_reduce_scatter(
        down_out.reshape(capacity, row_count, -1, model_width)
    )
    returned = lax.all_to_all(summed, VOCAB_AXES, split_axis=1, concat_axis=1, tiled=True)
    combine = selector * weights.T[:, None, :]
    moe_sum = jnp.einsum(
        "esr,sed->rd", combine, returned.astype(jnp.float32), precision=lax.Precision.HIGHEST
    )
    mixed_rows = resid_in + moe_sum
    final_normed = rms_norm(mixed_rows, head_gain).astype(jnp.bfloat16)
    padded = -(-rows_dev // 16) * 16
    block = jnp.concatenate(
        [final_normed, jnp.zeros((padded - rows_dev, model_width), final_normed.dtype)]
    )
    gathered = lax.all_gather(block, ALL_AXES, axis=0, tiled=True)
    devices = gathered.shape[0] // padded
    logits = lax.dot_general(
        gathered, head, (((1,), (1,)), ((), ())), preferred_element_type=jnp.float32
    )
    target_logits = logits.reshape(devices, padded, local_vocab)
    halves = rows_dev // slot_total

    def to_requests(values):
        return values[:, :rows_dev].reshape(requests, slot_total)

    def from_requests(values, fill):
        grid = values.reshape(devices, rows_dev)
        return jnp.concatenate(
            [grid, jnp.full((devices, padded - rows_dev), fill, grid.dtype)], axis=1
        )

    ids_t = from_requests(
        jnp.concatenate([local_ids, jnp.full((requests, 1), -1, jnp.int32)], axis=1), -1
    )
    id_match_t = jnp.arange(local_vocab, dtype=jnp.int32) == ids_t[..., None]
    pick_target = to_requests(jnp.sum(jnp.where(id_match_t, target_logits, 0.0), axis=-1))
    local_top_t = jnp.max(target_logits, axis=-1)
    local_sum_target = to_requests(
        jnp.sum(jnp.exp(target_logits - local_top_t[..., None]), axis=-1)
    )
    local_top_target = to_requests(local_top_t)
    tops, sums, picks = merged_stats(
        jnp.concatenate([local_top_target, local_top_draft], axis=1),
        jnp.concatenate([local_sum_target, local_sum_draft], axis=1),
        jnp.concatenate([pick_target, local_pick_draft], axis=1),
    )
    top_target, top_draft = tops[:, :slot_total], tops[:, slot_total:]
    sum_target, sum_draft = sums[:, :slot_total], sums[:, slot_total:]
    pick_t, pick_d = picks[:, :DRAFTS], picks[:, slot_total:]
    draft_exp = jnp.exp(draft_vals - top_draft[:, :, None])
    draft_prob = draft_exp / sum_draft[:, :, None]
    log_target = pick_t - top_target[:, :DRAFTS] - jnp.log(sum_target[:, :DRAFTS])
    log_draft = pick_d - top_draft - jnp.log(sum_draft)
    accept = jnp.exp(jnp.minimum(log_target - log_draft, 0.0))
    position = (jnp.arange(slot_total, dtype=jnp.int32)[None, :] == reject_pos[:, None]).astype(
        jnp.float32
    )
    weight_t = from_requests(position / sum_target, 0.0)
    weighted = weight_t[..., None] * jnp.exp(
        target_logits - from_requests(top_target, 0.0)[..., None]
    )
    target_at = jnp.stack(
        [
            jnp.sum(weighted[:, half * slot_total:(half + 1) * slot_total], axis=1)
            for half in range(halves)
        ],
        axis=1,
    ).reshape(requests, local_vocab)
    draft_at = jnp.sum(position[:, :DRAFTS, None] * draft_prob, axis=1)
    gap_rows = jnp.maximum(target_at - draft_at, 0.0)
    gap_total = gathered_sum(jnp.sum(gap_rows, axis=-1))
    residual = jnp.sqrt(V * gap_rows / gap_total[:, None])
    return (residual, accept)


def solution(mesh):
    row_size, vocab_size = mesh.devices.shape
    split = (row_size, 4, vocab_size // 8, 2)
    fine = Mesh(np.asarray(mesh.devices).reshape(split), ALL_AXES)
    spread = ALL_AXES
    placed = (
        P(spread, None),
        P(),
        P(),
        P(spread, None),
        P(VOCAB_AXES, None, "row"),
        P(VOCAB_AXES, None, "row"),
        P(VOCAB_AXES, "row", None),
        P(),
        P(spread, None),
        P(None, None, spread),
        P(),
        P(),
    )
    return jax.shard_map(
        body,
        mesh=fine,
        in_specs=placed,
        out_specs=(P(None, spread), P()),
        check_vma=False,
    )
```

```python
import jax
import jax.numpy as jnp
import numpy as np
from jax import lax
from jax.sharding import Mesh
from jax.sharding import PartitionSpec as P

V = 65536
DRAFTS = 4

VOCAB_AXES = ("vz", "vx", "core")
ALL_AXES = ("row",) + VOCAB_AXES


def rms_norm(values, gain):
    return values * lax.rsqrt(jnp.mean(values * values, axis=-1, keepdims=True) + 1e-06) * gain


def gather_groups():
    return (("row", "vz"), ("vx", "core"))


def merged_stats(top, total, pick):
    payload = jnp.stack([top, total, pick])
    for axes in gather_groups():
        every = lax.all_gather(payload, axes, axis=0, tiled=False)
        best = jnp.max(every[:, 0], axis=0)
        scaled = jnp.sum(every[:, 1] * jnp.exp(every[:, 0] - best[None]), axis=0)
        payload = jnp.stack([best, scaled, jnp.sum(every[:, 2], axis=0)])
    return payload[0], payload[1], payload[2]


def gathered_sum(values):
    for axes in gather_groups():
        values = jnp.sum(lax.all_gather(values, axes, axis=0, tiled=False), axis=0)
    return values


def row_reduce_scatter(parts):
    groups = parts.shape[1]
    me = lax.axis_index("row")
    total = lax.dynamic_index_in_dim(parts, me, axis=1, keepdims=False).astype(jnp.float32)
    for shift in range(1, groups):
        chunk = lax.dynamic_index_in_dim(parts, (me + shift) % groups, axis=1, keepdims=False)
        pairs = [(i, (i + shift) % groups) for i in range(groups)]
        total = total + lax.ppermute(chunk, "row", pairs).astype(jnp.float32)
    return total.astype(jnp.bfloat16)


def body(
    tokens,
    norm_gain,
    router,
    routes,
    w_gate,
    w_up,
    w_down,
    head_gain,
    head,
    draft_logits,
    draft_tokens,
    reject_pos,
):
    vocab_count = 1
    for axis in VOCAB_AXES:
        vocab_count *= lax.axis_size(axis)
    row_count = lax.axis_size("row")
    rows_dev = tokens.shape[0]
    model_width = tokens.shape[1]
    top_k = routes.shape[1]
    experts = w_gate.shape[0] * vocab_count
    capacity = min(rows_dev, (rows_dev * top_k + experts - 1) // experts)
    local_vocab = head.shape[0]
    requests = draft_tokens.shape[0]
    slot_total = DRAFTS + 1
    offset = lax.axis_index(ALL_AXES) * local_vocab
    local_ids = draft_tokens - offset
    id_match = jnp.arange(local_vocab, dtype=jnp.int32)[None, None, :] == local_ids[:, :, None]

    draft_vals = draft_logits.astype(jnp.float32)
    local_top_draft = jnp.max(draft_vals, axis=-1)
    local_sum_draft = jnp.sum(jnp.exp(draft_vals - local_top_draft[:, :, None]), axis=-1)
    local_pick_draft = jnp.sum(jnp.where(id_match, draft_vals, 0.0), axis=-1)

    resid_in = tokens.astype(jnp.float32)
    normed = rms_norm(resid_in, norm_gain).astype(jnp.bfloat16)
    scores = jax.nn.sigmoid(jnp.dot(normed, router, preferred_element_type=jnp.float32))
    member = routes[:, :, None] == jnp.arange(experts, dtype=jnp.int32)[None, None, :]
    chosen = jnp.any(member, axis=1)
    chosen_int = chosen.astype(jnp.int32)
    picked = chosen.astype(jnp.float32) * scores
    weights = 2.5 * picked / jnp.sum(picked, axis=1, keepdims=True)
    earlier = jnp.cumsum(chosen_int, axis=0) - chosen_int
    slot_ids = jnp.arange(capacity, dtype=jnp.int32)[None, :, None]
    selector = ((earlier.T[:, None, :] == slot_ids) & chosen.T[:, None, :]).astype(jnp.float32)
    send_buffer = jnp.einsum(
        "esr,rd->sed", selector.astype(jnp.bfloat16), normed, preferred_element_type=jnp.float32
    ).astype(jnp.bfloat16)
    gate_w = w_gate[0]
    up_w = w_up[0]
    down_w = w_down[0]
    received = lax.all_to_all(send_buffer, VOCAB_AXES, split_axis=1, concat_axis=1, tiled=True)
    shard_piece = lax.all_gather(received, "row", axis=1, tiled=True)
    flat_rows = shard_piece.reshape(-1, model_width)
    gate_out = jnp.dot(flat_rows, gate_w, preferred_element_type=jnp.float32)
    up_out = jnp.dot(flat_rows, up_w, preferred_element_type=jnp.float32)
    hidden = (jax.nn.silu(gate_out) * up_out).astype(jnp.bfloat16)
    down_out = jnp.dot(hidden, down_w, preferred_element_type=jnp.float32).astype(jnp.bfloat16)
    summed = row_reduce_scatter(
        down_out.reshape(capacity, row_count, -1, model_width)
    )
    returned = lax.all_to_all(summed, VOCAB_AXES, split_axis=1, concat_axis=1, tiled=True)
    combine = selector * weights.T[:, None, :]
    moe_sum = jnp.einsum(
        "esr,sed->rd", combine, returned.astype(jnp.float32), precision=lax.Precision.HIGHEST
    )
    mixed_rows = resid_in + moe_sum
    final_normed = rms_norm(mixed_rows, head_gain).astype(jnp.bfloat16)
    padded = -(-rows_dev // 16) * 16
    block = jnp.concatenate(
        [final_normed, jnp.zeros((padded - rows_dev, model_width), final_normed.dtype)]
    )
    gather_axes = ALL_AXES[::-1]
    sizes = [lax.axis_size(axis) for axis in gather_axes]
    back = tuple(range(len(sizes) - 1, -1, -1))
    gathered = lax.all_gather(block, gather_axes, axis=0, tiled=True)
    devices = gathered.shape[0] // padded
    logits = lax.dot_general(
        gathered, head, (((1,), (1,)), ((), ())), preferred_element_type=jnp.float32
    )
    target_logits = logits.reshape(devices, padded, local_vocab)
    halves = rows_dev // slot_total

    def natural(values):
        rest = values.shape[1:]
        grid = values.reshape(tuple(sizes) + rest)
        order = back + tuple(range(len(sizes), grid.ndim))
        return jnp.transpose(grid, order).reshape(values.shape)

    def gathered_order(values):
        rest = values.shape[1:]
        grid = values.reshape(tuple(sizes[::-1]) + rest)
        order = back + tuple(range(len(sizes), grid.ndim))
        return jnp.transpose(grid, order).reshape(values.shape)

    def to_requests(values):
        return natural(values[:, :rows_dev]).reshape(requests, slot_total)

    def from_requests(values, fill):
        grid = gathered_order(values.reshape(devices, rows_dev))
        return jnp.concatenate(
            [grid, jnp.full((devices, padded - rows_dev), fill, grid.dtype)], axis=1
        )

    ids_t = from_requests(
        jnp.concatenate([local_ids, jnp.full((requests, 1), -1, jnp.int32)], axis=1), -1
    )
    id_match_t = jnp.arange(local_vocab, dtype=jnp.int32) == ids_t[..., None]
    pick_target = to_requests(jnp.sum(jnp.where(id_match_t, target_logits, 0.0), axis=-1))
    local_top_t = jnp.max(target_logits, axis=-1)
    local_sum_target = to_requests(
        jnp.sum(jnp.exp(target_logits - local_top_t[..., None]), axis=-1)
    )
    local_top_target = to_requests(local_top_t)
    tops, sums, picks = merged_stats(
        jnp.concatenate([local_top_target, local_top_draft], axis=1),
        jnp.concatenate([local_sum_target, local_sum_draft], axis=1),
        jnp.concatenate([pick_target, local_pick_draft], axis=1),
    )
    top_target, top_draft = tops[:, :slot_total], tops[:, slot_total:]
    sum_target, sum_draft = sums[:, :slot_total], sums[:, slot_total:]
    pick_t, pick_d = picks[:, :DRAFTS], picks[:, slot_total:]
    draft_exp = jnp.exp(draft_vals - top_draft[:, :, None])
    draft_prob = draft_exp / sum_draft[:, :, None]
    log_target = pick_t - top_target[:, :DRAFTS] - jnp.log(sum_target[:, :DRAFTS])
    log_draft = pick_d - top_draft - jnp.log(sum_draft)
    accept = jnp.exp(jnp.minimum(log_target - log_draft, 0.0))
    position = (jnp.arange(slot_total, dtype=jnp.int32)[None, :] == reject_pos[:, None]).astype(
        jnp.float32
    )
    weight_t = from_requests(position / sum_target, 0.0)
    weighted = weight_t[..., None] * jnp.exp(
        target_logits - from_requests(top_target, 0.0)[..., None]
    )
    target_at = jnp.stack(
        [
            jnp.sum(weighted[:, half * slot_total:(half + 1) * slot_total], axis=1)
            for half in range(halves)
        ],
        axis=1,
    )
    target_at = natural(target_at).reshape(requests, local_vocab)
    draft_at = jnp.sum(position[:, :DRAFTS, None] * draft_prob, axis=1)
    gap_rows = jnp.maximum(target_at - draft_at, 0.0)
    gap_total = gathered_sum(jnp.sum(gap_rows, axis=-1))
    residual = jnp.sqrt(V * gap_rows / gap_total[:, None])
    return (residual, accept)


def solution(mesh):
    row_size, vocab_size = mesh.devices.shape
    split = (row_size, 4, vocab_size // 8, 2)
    fine = Mesh(np.asarray(mesh.devices).reshape(split), ALL_AXES)
    spread = ALL_AXES
    placed = (
        P(spread, None),
        P(),
        P(),
        P(spread, None),
        P(VOCAB_AXES, None, "row"),
        P(VOCAB_AXES, None, "row"),
        P(VOCAB_AXES, "row", None),
        P(),
        P(spread, None),
        P(None, None, spread),
        P(),
        P(),
    )
    return jax.shard_map(
        body,
        mesh=fine,
        in_specs=placed,
        out_specs=(P(None, spread), P()),
        check_vma=False,
    )
```

```python
import jax
import jax.numpy as jnp
import numpy as np
from jax import lax
from jax.sharding import Mesh
from jax.sharding import PartitionSpec as P

V = 65536
DRAFTS = 4

VOCAB_AXES = ("vz", "vx", "core")
ALL_AXES = ("row",) + VOCAB_AXES


def rms_norm(values, gain):
    return values * lax.rsqrt(jnp.mean(values * values, axis=-1, keepdims=True) + 1e-06) * gain


def gather_groups():
    return (("row", "vz"), ("vx", "core"))


def merged_stats(top, total, pick):
    payload = jnp.stack([top, total, pick])
    for axes in gather_groups():
        every = lax.all_gather(payload, axes, axis=0, tiled=False)
        best = jnp.max(every[:, 0], axis=0)
        scaled = jnp.sum(every[:, 1] * jnp.exp(every[:, 0] - best[None]), axis=0)
        payload = jnp.stack([best, scaled, jnp.sum(every[:, 2], axis=0)])
    return payload[0], payload[1], payload[2]


def gathered_sum(values):
    for axes in gather_groups():
        values = jnp.sum(lax.all_gather(values, axes, axis=0, tiled=False), axis=0)
    return values


def row_reduce_scatter(parts):
    groups = parts.shape[1]
    me = lax.axis_index("row")
    total = lax.dynamic_index_in_dim(parts, me, axis=1, keepdims=False).astype(jnp.float32)
    for shift in range(1, groups):
        chunk = lax.dynamic_index_in_dim(parts, (me + shift) % groups, axis=1, keepdims=False)
        pairs = [(i, (i + shift) % groups) for i in range(groups)]
        total = total + lax.ppermute(chunk, "row", pairs).astype(jnp.float32)
    return total.astype(jnp.bfloat16)


def body(
    tokens,
    norm_gain,
    router,
    routes,
    w_gate,
    w_up,
    w_down,
    head_gain,
    head,
    draft_logits,
    draft_tokens,
    reject_pos,
):
    vocab_count = 1
    for axis in VOCAB_AXES:
        vocab_count *= lax.axis_size(axis)
    row_count = lax.axis_size("row")
    rows_dev = tokens.shape[0]
    model_width = tokens.shape[1]
    top_k = routes.shape[1]
    experts = w_gate.shape[0] * vocab_count
    capacity = min(rows_dev, (rows_dev * top_k + experts - 1) // experts)
    local_vocab = head.shape[0]
    requests = draft_tokens.shape[0]
    slot_total = DRAFTS + 1
    offset = lax.axis_index(ALL_AXES) * local_vocab
    local_ids = draft_tokens - offset
    id_match = jnp.arange(local_vocab, dtype=jnp.int32)[None, None, :] == local_ids[:, :, None]

    draft_vals = draft_logits.astype(jnp.float32)
    local_top_draft = jnp.max(draft_vals, axis=-1)
    local_sum_draft = jnp.sum(jnp.exp(draft_vals - local_top_draft[:, :, None]), axis=-1)
    local_pick_draft = jnp.sum(jnp.where(id_match, draft_vals, 0.0), axis=-1)

    resid_in = tokens.astype(jnp.float32)
    normed = rms_norm(resid_in, norm_gain).astype(jnp.bfloat16)
    scores = jax.nn.sigmoid(jnp.dot(normed, router, preferred_element_type=jnp.float32))
    member = routes[:, :, None] == jnp.arange(experts, dtype=jnp.int32)[None, None, :]
    chosen = jnp.any(member, axis=1)
    chosen_int = chosen.astype(jnp.int32)
    picked = chosen.astype(jnp.float32) * scores
    weights = 2.5 * picked / jnp.sum(picked, axis=1, keepdims=True)
    earlier = jnp.cumsum(chosen_int, axis=0) - chosen_int
    slot_ids = jnp.arange(capacity, dtype=jnp.int32)[None, :, None]
    selector = ((earlier.T[:, None, :] == slot_ids) & chosen.T[:, None, :]).astype(jnp.float32)
    per_expert = capacity * model_width
    fold = 4 if per_expert % (4 * 128) == 0 else capacity
    send_buffer = jnp.einsum(
        "esr,rd->esd", selector.astype(jnp.bfloat16), normed, preferred_element_type=jnp.float32
    ).astype(jnp.bfloat16)
    gate_w = w_gate[0]
    up_w = w_up[0]
    down_w = w_down[0]

    def exchange(buffer):
        folded = buffer.reshape(buffer.shape[0], fold, per_expert // fold)
        moved = lax.all_to_all(folded, VOCAB_AXES, split_axis=0, concat_axis=0, tiled=True)
        return moved.reshape(buffer.shape)

    received = jnp.transpose(exchange(send_buffer), (1, 0, 2))
    shard_piece = lax.all_gather(received, "row", axis=1, tiled=True)
    flat_rows = shard_piece.reshape(-1, model_width)
    gate_out = jnp.dot(flat_rows, gate_w, preferred_element_type=jnp.float32)
    up_out = jnp.dot(flat_rows, up_w, preferred_element_type=jnp.float32)
    hidden = (jax.nn.silu(gate_out) * up_out).astype(jnp.bfloat16)
    down_out = jnp.dot(hidden, down_w, preferred_element_type=jnp.float32).astype(jnp.bfloat16)
    summed = row_reduce_scatter(
        down_out.reshape(capacity, row_count, -1, model_width)
    )
    returned = exchange(jnp.transpose(summed, (1, 0, 2)))
    combine = selector * weights.T[:, None, :]
    moe_sum = jnp.einsum(
        "esr,esd->rd", combine, returned.astype(jnp.float32), precision=lax.Precision.HIGHEST
    )
    mixed_rows = resid_in + moe_sum
    final_normed = rms_norm(mixed_rows, head_gain).astype(jnp.bfloat16)
    padded = -(-rows_dev // 16) * 16
    block = jnp.concatenate(
        [final_normed, jnp.zeros((padded - rows_dev, model_width), final_normed.dtype)]
    )
    gathered = lax.all_gather(block, ALL_AXES, axis=0, tiled=True)
    devices = gathered.shape[0] // padded
    logits = lax.dot_general(
        gathered, head, (((1,), (1,)), ((), ())), preferred_element_type=jnp.float32
    )
    target_logits = logits.reshape(devices, padded, local_vocab)
    halves = rows_dev // slot_total

    def to_requests(values):
        return values[:, :rows_dev].reshape(requests, slot_total)

    def from_requests(values, fill):
        grid = values.reshape(devices, rows_dev)
        return jnp.concatenate(
            [grid, jnp.full((devices, padded - rows_dev), fill, grid.dtype)], axis=1
        )

    ids_t = from_requests(
        jnp.concatenate([local_ids, jnp.full((requests, 1), -1, jnp.int32)], axis=1), -1
    )
    id_match_t = jnp.arange(local_vocab, dtype=jnp.int32) == ids_t[..., None]
    pick_target = to_requests(jnp.sum(jnp.where(id_match_t, target_logits, 0.0), axis=-1))
    local_top_t = jnp.max(target_logits, axis=-1)
    local_sum_target = to_requests(
        jnp.sum(jnp.exp(target_logits - local_top_t[..., None]), axis=-1)
    )
    local_top_target = to_requests(local_top_t)
    tops, sums, picks = merged_stats(
        jnp.concatenate([local_top_target, local_top_draft], axis=1),
        jnp.concatenate([local_sum_target, local_sum_draft], axis=1),
        jnp.concatenate([pick_target, local_pick_draft], axis=1),
    )
    top_target, top_draft = tops[:, :slot_total], tops[:, slot_total:]
    sum_target, sum_draft = sums[:, :slot_total], sums[:, slot_total:]
    pick_t, pick_d = picks[:, :DRAFTS], picks[:, slot_total:]
    draft_exp = jnp.exp(draft_vals - top_draft[:, :, None])
    draft_prob = draft_exp / sum_draft[:, :, None]
    log_target = pick_t - top_target[:, :DRAFTS] - jnp.log(sum_target[:, :DRAFTS])
    log_draft = pick_d - top_draft - jnp.log(sum_draft)
    accept = jnp.exp(jnp.minimum(log_target - log_draft, 0.0))
    position = (jnp.arange(slot_total, dtype=jnp.int32)[None, :] == reject_pos[:, None]).astype(
        jnp.float32
    )
    weight_t = from_requests(position / sum_target, 0.0)
    weighted = weight_t[..., None] * jnp.exp(
        target_logits - from_requests(top_target, 0.0)[..., None]
    )
    target_at = jnp.stack(
        [
            jnp.sum(weighted[:, half * slot_total:(half + 1) * slot_total], axis=1)
            for half in range(halves)
        ],
        axis=1,
    ).reshape(requests, local_vocab)
    draft_at = jnp.sum(position[:, :DRAFTS, None] * draft_prob, axis=1)
    gap_rows = jnp.maximum(target_at - draft_at, 0.0)
    gap_total = gathered_sum(jnp.sum(gap_rows, axis=-1))
    residual = jnp.sqrt(V * gap_rows / gap_total[:, None])
    return (residual, accept)


def solution(mesh):
    row_size, vocab_size = mesh.devices.shape
    split = (row_size, 4, vocab_size // 8, 2)
    fine = Mesh(np.asarray(mesh.devices).reshape(split), ALL_AXES)
    spread = ALL_AXES
    placed = (
        P(spread, None),
        P(),
        P(),
        P(spread, None),
        P(VOCAB_AXES, None, "row"),
        P(VOCAB_AXES, None, "row"),
        P(VOCAB_AXES, "row", None),
        P(),
        P(spread, None),
        P(None, None, spread),
        P(),
        P(),
    )
    return jax.shard_map(
        body,
        mesh=fine,
        in_specs=placed,
        out_specs=(P(None, spread), P()),
        check_vma=False,
    )
```

```python
import jax
import jax.numpy as jnp
import numpy as np
from jax import lax
from jax.sharding import Mesh
from jax.sharding import PartitionSpec as P

V = 65536
DRAFTS = 4

VOCAB_AXES = ("vz", "vx", "core")
ALL_AXES = ("row",) + VOCAB_AXES


def rms_norm(values, gain):
    return values * lax.rsqrt(jnp.mean(values * values, axis=-1, keepdims=True) + 1e-06) * gain


def gather_groups():
    return (("row", "vz"), ("vx", "core"))


def merged_stats(top, total, pick):
    payload = jnp.stack([top, total, pick])
    for axes in gather_groups():
        every = lax.all_gather(payload, axes, axis=0, tiled=False)
        best = jnp.max(every[:, 0], axis=0)
        scaled = jnp.sum(every[:, 1] * jnp.exp(every[:, 0] - best[None]), axis=0)
        payload = jnp.stack([best, scaled, jnp.sum(every[:, 2], axis=0)])
    return payload[0], payload[1], payload[2]


def gathered_sum(values):
    return jnp.sum(lax.all_gather(values, ALL_AXES, axis=0, tiled=False), axis=0)


def row_reduce_scatter(parts):
    groups = parts.shape[1]
    me = lax.axis_index("row")
    total = lax.dynamic_index_in_dim(parts, me, axis=1, keepdims=False).astype(jnp.float32)
    for shift in range(1, groups):
        chunk = lax.dynamic_index_in_dim(parts, (me + shift) % groups, axis=1, keepdims=False)
        pairs = [(i, (i + shift) % groups) for i in range(groups)]
        total = total + lax.ppermute(chunk, "row", pairs).astype(jnp.float32)
    return total.astype(jnp.bfloat16)


def body(
    tokens,
    norm_gain,
    router,
    routes,
    w_gate,
    w_up,
    w_down,
    head_gain,
    head,
    draft_logits,
    draft_tokens,
    reject_pos,
):
    vocab_count = 1
    for axis in VOCAB_AXES:
        vocab_count *= lax.axis_size(axis)
    row_count = lax.axis_size("row")
    rows_dev = tokens.shape[0]
    model_width = tokens.shape[1]
    top_k = routes.shape[1]
    experts = w_gate.shape[0] * vocab_count
    capacity = min(rows_dev, (rows_dev * top_k + experts - 1) // experts)
    local_vocab = head.shape[0]
    requests = draft_tokens.shape[0]
    slot_total = DRAFTS + 1
    offset = lax.axis_index(ALL_AXES) * local_vocab
    local_ids = draft_tokens - offset
    id_match = jnp.arange(local_vocab, dtype=jnp.int32)[None, None, :] == local_ids[:, :, None]

    draft_vals = draft_logits.astype(jnp.float32)
    local_top_draft = jnp.max(draft_vals, axis=-1)
    local_sum_draft = jnp.sum(jnp.exp(draft_vals - local_top_draft[:, :, None]), axis=-1)
    local_pick_draft = jnp.sum(jnp.where(id_match, draft_vals, 0.0), axis=-1)

    resid_in = tokens.astype(jnp.float32)
    normed = rms_norm(resid_in, norm_gain).astype(jnp.bfloat16)
    scores = jax.nn.sigmoid(jnp.dot(normed, router, preferred_element_type=jnp.float32))
    member = routes[:, :, None] == jnp.arange(experts, dtype=jnp.int32)[None, None, :]
    chosen = jnp.any(member, axis=1)
    chosen_int = chosen.astype(jnp.int32)
    picked = chosen.astype(jnp.float32) * scores
    weights = 2.5 * picked / jnp.sum(picked, axis=1, keepdims=True)
    earlier = jnp.cumsum(chosen_int, axis=0) - chosen_int
    slot_ids = jnp.arange(capacity, dtype=jnp.int32)[None, :, None]
    selector = ((earlier.T[:, None, :] == slot_ids) & chosen.T[:, None, :]).astype(jnp.float32)
    send_buffer = jnp.einsum(
        "esr,rd->sed", selector.astype(jnp.bfloat16), normed, preferred_element_type=jnp.float32
    ).astype(jnp.bfloat16)
    gate_w = w_gate[0]
    up_w = w_up[0]
    down_w = w_down[0]
    received = lax.all_to_all(send_buffer, VOCAB_AXES, split_axis=1, concat_axis=1, tiled=True)
    shard_piece = lax.all_gather(received, "row", axis=1, tiled=True)
    flat_rows = shard_piece.reshape(-1, model_width)
    gate_out = jnp.dot(flat_rows, gate_w, preferred_element_type=jnp.float32)
    up_out = jnp.dot(flat_rows, up_w, preferred_element_type=jnp.float32)
    hidden = (jax.nn.silu(gate_out) * up_out).astype(jnp.bfloat16)
    down_out = jnp.dot(hidden, down_w, preferred_element_type=jnp.float32).astype(jnp.bfloat16)
    summed = row_reduce_scatter(
        down_out.reshape(capacity, row_count, -1, model_width)
    )
    returned = lax.all_to_all(summed, VOCAB_AXES, split_axis=1, concat_axis=1, tiled=True)
    combine = selector * weights.T[:, None, :]
    moe_sum = jnp.einsum(
        "esr,sed->rd", combine, returned.astype(jnp.float32), precision=lax.Precision.HIGHEST
    )
    mixed_rows = resid_in + moe_sum
    final_normed = rms_norm(mixed_rows, head_gain).astype(jnp.bfloat16)
    padded = -(-rows_dev // 16) * 16
    block = jnp.concatenate(
        [final_normed, jnp.zeros((padded - rows_dev, model_width), final_normed.dtype)]
    )
    gathered = lax.all_gather(block, ALL_AXES, axis=0, tiled=True)
    devices = gathered.shape[0] // padded
    logits = lax.dot_general(
        gathered, head, (((1,), (1,)), ((), ())), preferred_element_type=jnp.float32
    )
    target_logits = logits.reshape(devices, padded, local_vocab)
    halves = rows_dev // slot_total

    def to_requests(values):
        return values[:, :rows_dev].reshape(requests, slot_total)

    def from_requests(values, fill):
        grid = values.reshape(devices, rows_dev)
        return jnp.concatenate(
            [grid, jnp.full((devices, padded - rows_dev), fill, grid.dtype)], axis=1
        )

    ids_t = from_requests(
        jnp.concatenate([local_ids, jnp.full((requests, 1), -1, jnp.int32)], axis=1), -1
    )
    id_match_t = jnp.arange(local_vocab, dtype=jnp.int32) == ids_t[..., None]
    pick_target = to_requests(jnp.sum(jnp.where(id_match_t, target_logits, 0.0), axis=-1))
    local_top_t = jnp.max(target_logits, axis=-1)
    local_sum_target = to_requests(
        jnp.sum(jnp.exp(target_logits - local_top_t[..., None]), axis=-1)
    )
    local_top_target = to_requests(local_top_t)
    tops, sums, picks = merged_stats(
        jnp.concatenate([local_top_target, local_top_draft], axis=1),
        jnp.concatenate([local_sum_target, local_sum_draft], axis=1),
        jnp.concatenate([pick_target, local_pick_draft], axis=1),
    )
    top_target, top_draft = tops[:, :slot_total], tops[:, slot_total:]
    sum_target, sum_draft = sums[:, :slot_total], sums[:, slot_total:]
    pick_t, pick_d = picks[:, :DRAFTS], picks[:, slot_total:]
    draft_exp = jnp.exp(draft_vals - top_draft[:, :, None])
    draft_prob = draft_exp / sum_draft[:, :, None]
    log_target = pick_t - top_target[:, :DRAFTS] - jnp.log(sum_target[:, :DRAFTS])
    log_draft = pick_d - top_draft - jnp.log(sum_draft)
    accept = jnp.exp(jnp.minimum(log_target - log_draft, 0.0))
    position = (jnp.arange(slot_total, dtype=jnp.int32)[None, :] == reject_pos[:, None]).astype(
        jnp.float32
    )
    weight_t = from_requests(position / sum_target, 0.0)
    weighted = weight_t[..., None] * jnp.exp(
        target_logits - from_requests(top_target, 0.0)[..., None]
    )
    target_at = jnp.stack(
        [
            jnp.sum(weighted[:, half * slot_total:(half + 1) * slot_total], axis=1)
            for half in range(halves)
        ],
        axis=1,
    ).reshape(requests, local_vocab)
    draft_at = jnp.sum(position[:, :DRAFTS, None] * draft_prob, axis=1)
    gap_rows = jnp.maximum(target_at - draft_at, 0.0)
    gap_total = gathered_sum(jnp.sum(gap_rows, axis=-1))
    residual = jnp.sqrt(V * gap_rows / gap_total[:, None])
    return (residual, accept)


def solution(mesh):
    row_size, vocab_size = mesh.devices.shape
    split = (row_size, 4, vocab_size // 8, 2)
    fine = Mesh(np.asarray(mesh.devices).reshape(split), ALL_AXES)
    spread = ALL_AXES
    placed = (
        P(spread, None),
        P(),
        P(),
        P(spread, None),
        P(VOCAB_AXES, None, "row"),
        P(VOCAB_AXES, None, "row"),
        P(VOCAB_AXES, "row", None),
        P(),
        P(spread, None),
        P(None, None, spread),
        P(),
        P(),
    )
    return jax.shard_map(
        body,
        mesh=fine,
        in_specs=placed,
        out_specs=(P(None, spread), P()),
        check_vma=False,
    )
```

```python
import jax
import jax.numpy as jnp
import numpy as np
from jax import lax
from jax.sharding import Mesh
from jax.sharding import PartitionSpec as P

V = 65536
DRAFTS = 4

VOCAB_AXES = ("vz", "vx", "core")
ALL_AXES = ("row",) + VOCAB_AXES


def rms_norm(values, gain):
    return values * lax.rsqrt(jnp.mean(values * values, axis=-1, keepdims=True) + 1e-06) * gain


def gather_groups():
    return (("vx", "core"), ("row", "vz"))


def merged_stats(top, total, pick):
    payload = jnp.stack([top, total, pick])
    for axes in gather_groups():
        every = lax.all_gather(payload, axes, axis=0, tiled=False)
        best = jnp.max(every[:, 0], axis=0)
        scaled = jnp.sum(every[:, 1] * jnp.exp(every[:, 0] - best[None]), axis=0)
        payload = jnp.stack([best, scaled, jnp.sum(every[:, 2], axis=0)])
    return payload[0], payload[1], payload[2]


def gathered_sum(values):
    for axes in gather_groups():
        values = jnp.sum(lax.all_gather(values, axes, axis=0, tiled=False), axis=0)
    return values


def row_reduce_scatter(parts):
    groups = parts.shape[1]
    me = lax.axis_index("row")
    total = lax.dynamic_index_in_dim(parts, me, axis=1, keepdims=False).astype(jnp.float32)
    for shift in range(1, groups):
        chunk = lax.dynamic_index_in_dim(parts, (me + shift) % groups, axis=1, keepdims=False)
        pairs = [(i, (i + shift) % groups) for i in range(groups)]
        total = total + lax.ppermute(chunk, "row", pairs).astype(jnp.float32)
    return total.astype(jnp.bfloat16)


def body(
    tokens,
    norm_gain,
    router,
    routes,
    w_gate,
    w_up,
    w_down,
    head_gain,
    head,
    draft_logits,
    draft_tokens,
    reject_pos,
):
    vocab_count = 1
    for axis in VOCAB_AXES:
        vocab_count *= lax.axis_size(axis)
    row_count = lax.axis_size("row")
    rows_dev = tokens.shape[0]
    model_width = tokens.shape[1]
    top_k = routes.shape[1]
    experts = w_gate.shape[0] * vocab_count
    capacity = min(rows_dev, (rows_dev * top_k + experts - 1) // experts)
    local_vocab = head.shape[0]
    requests = draft_tokens.shape[0]
    slot_total = DRAFTS + 1
    offset = lax.axis_index(ALL_AXES) * local_vocab
    local_ids = draft_tokens - offset
    id_match = jnp.arange(local_vocab, dtype=jnp.int32)[None, None, :] == local_ids[:, :, None]

    draft_vals = draft_logits.astype(jnp.float32)
    local_top_draft = jnp.max(draft_vals, axis=-1)
    local_sum_draft = jnp.sum(jnp.exp(draft_vals - local_top_draft[:, :, None]), axis=-1)
    local_pick_draft = jnp.sum(jnp.where(id_match, draft_vals, 0.0), axis=-1)

    resid_in = tokens.astype(jnp.float32)
    normed = rms_norm(resid_in, norm_gain).astype(jnp.bfloat16)
    scores = jax.nn.sigmoid(jnp.dot(normed, router, preferred_element_type=jnp.float32))
    member = routes[:, :, None] == jnp.arange(experts, dtype=jnp.int32)[None, None, :]
    chosen = jnp.any(member, axis=1)
    chosen_int = chosen.astype(jnp.int32)
    picked = chosen.astype(jnp.float32) * scores
    weights = 2.5 * picked / jnp.sum(picked, axis=1, keepdims=True)
    earlier = jnp.cumsum(chosen_int, axis=0) - chosen_int
    slot_ids = jnp.arange(capacity, dtype=jnp.int32)[None, :, None]
    selector = ((earlier.T[:, None, :] == slot_ids) & chosen.T[:, None, :]).astype(jnp.float32)
    send_buffer = jnp.einsum(
        "esr,rd->sed", selector.astype(jnp.bfloat16), normed, preferred_element_type=jnp.float32
    ).astype(jnp.bfloat16)
    gate_w = w_gate[0]
    up_w = w_up[0]
    down_w = w_down[0]
    received = lax.all_to_all(send_buffer, VOCAB_AXES, split_axis=1, concat_axis=1, tiled=True)
    shard_piece = lax.all_gather(received, "row", axis=1, tiled=True)
    flat_rows = shard_piece.reshape(-1, model_width)
    gate_out = jnp.dot(flat_rows, gate_w, preferred_element_type=jnp.float32)
    up_out = jnp.dot(flat_rows, up_w, preferred_element_type=jnp.float32)
    hidden = (jax.nn.silu(gate_out) * up_out).astype(jnp.bfloat16)
    down_out = jnp.dot(hidden, down_w, preferred_element_type=jnp.float32).astype(jnp.bfloat16)
    summed = row_reduce_scatter(
        down_out.reshape(capacity, row_count, -1, model_width)
    )
    returned = lax.all_to_all(summed, VOCAB_AXES, split_axis=1, concat_axis=1, tiled=True)
    combine = selector * weights.T[:, None, :]
    moe_sum = jnp.einsum(
        "esr,sed->rd", combine, returned.astype(jnp.float32), precision=lax.Precision.HIGHEST
    )
    mixed_rows = resid_in + moe_sum
    final_normed = rms_norm(mixed_rows, head_gain).astype(jnp.bfloat16)
    padded = -(-rows_dev // 16) * 16
    block = jnp.concatenate(
        [final_normed, jnp.zeros((padded - rows_dev, model_width), final_normed.dtype)]
    )
    gathered = lax.all_gather(block, ALL_AXES, axis=0, tiled=True)
    devices = gathered.shape[0] // padded
    logits = lax.dot_general(
        gathered, head, (((1,), (1,)), ((), ())), preferred_element_type=jnp.float32
    )
    target_logits = logits.reshape(devices, padded, local_vocab)
    halves = rows_dev // slot_total

    def to_requests(values):
        return values[:, :rows_dev].reshape(requests, slot_total)

    def from_requests(values, fill):
        grid = values.reshape(devices, rows_dev)
        return jnp.concatenate(
            [grid, jnp.full((devices, padded - rows_dev), fill, grid.dtype)], axis=1
        )

    ids_t = from_requests(
        jnp.concatenate([local_ids, jnp.full((requests, 1), -1, jnp.int32)], axis=1), -1
    )
    id_match_t = jnp.arange(local_vocab, dtype=jnp.int32) == ids_t[..., None]
    pick_target = to_requests(jnp.sum(jnp.where(id_match_t, target_logits, 0.0), axis=-1))
    local_top_t = jnp.max(target_logits, axis=-1)
    local_sum_target = to_requests(
        jnp.sum(jnp.exp(target_logits - local_top_t[..., None]), axis=-1)
    )
    local_top_target = to_requests(local_top_t)
    tops, sums, picks = merged_stats(
        jnp.concatenate([local_top_target, local_top_draft], axis=1),
        jnp.concatenate([local_sum_target, local_sum_draft], axis=1),
        jnp.concatenate([pick_target, local_pick_draft], axis=1),
    )
    top_target, top_draft = tops[:, :slot_total], tops[:, slot_total:]
    sum_target, sum_draft = sums[:, :slot_total], sums[:, slot_total:]
    pick_t, pick_d = picks[:, :DRAFTS], picks[:, slot_total:]
    draft_exp = jnp.exp(draft_vals - top_draft[:, :, None])
    draft_prob = draft_exp / sum_draft[:, :, None]
    log_target = pick_t - top_target[:, :DRAFTS] - jnp.log(sum_target[:, :DRAFTS])
    log_draft = pick_d - top_draft - jnp.log(sum_draft)
    accept = jnp.exp(jnp.minimum(log_target - log_draft, 0.0))
    position = (jnp.arange(slot_total, dtype=jnp.int32)[None, :] == reject_pos[:, None]).astype(
        jnp.float32
    )
    weight_t = from_requests(position / sum_target, 0.0)
    weighted = weight_t[..., None] * jnp.exp(
        target_logits - from_requests(top_target, 0.0)[..., None]
    )
    target_at = jnp.stack(
        [
            jnp.sum(weighted[:, half * slot_total:(half + 1) * slot_total], axis=1)
            for half in range(halves)
        ],
        axis=1,
    ).reshape(requests, local_vocab)
    draft_at = jnp.sum(position[:, :DRAFTS, None] * draft_prob, axis=1)
    gap_rows = jnp.maximum(target_at - draft_at, 0.0)
    gap_total = gathered_sum(jnp.sum(gap_rows, axis=-1))
    residual = jnp.sqrt(V * gap_rows / gap_total[:, None])
    return (residual, accept)


def solution(mesh):
    row_size, vocab_size = mesh.devices.shape
    split = (row_size, 4, vocab_size // 8, 2)
    fine = Mesh(np.asarray(mesh.devices).reshape(split), ALL_AXES)
    spread = ALL_AXES
    placed = (
        P(spread, None),
        P(),
        P(),
        P(spread, None),
        P(VOCAB_AXES, None, "row"),
        P(VOCAB_AXES, None, "row"),
        P(VOCAB_AXES, "row", None),
        P(),
        P(spread, None),
        P(None, None, spread),
        P(),
        P(),
    )
    return jax.shard_map(
        body,
        mesh=fine,
        in_specs=placed,
        out_specs=(P(None, spread), P()),
        check_vma=False,
    )
```
